32 devices in a mesh: dp: 8 (over z, y), region: 4 (over x, core).
Axes of the slice: x: 2, y: 2, z: 4, core: 2. Of those that a mesh axis runs over, the one named last changes fastest.
Arguments:
- travel_times: float32 [512, 128], P('dp'), may hold values from -60 to 60
- sensitivity: bfloat16 [512, 8, 128, 128], P('dp', 'region'), may hold values from -0.1875 to 0.1875
- tile_blocks: int32 [512, 8], P('dp', 'region'), may hold values from 0 to 1023
- face_blocks: int32 [1024, 2], P(('dp', 'region')), may hold values from 0 to 1023, as said below
- face_weights: float32 [1024, 128], P(('dp', 'region')), may hold values from 0.2 to 2
- face_count: int32 [32], P(('dp', 'region')), may hold values from 8 to 32, as said below
Outputs:
- solution: float32 [1024, 128], P('region')
The draws below stay inside these ranges and needn't reach their ends.
Inputs may be any that keep to these rules, and one draw needn't show every extreme that they name: `face_blocks`: the first block of a face lies in the region of the device that holds the face, the second in that region or in the region one step up or down, the regions closing into a loop. `face_count`: entry k counts the faces in use among the 32 rows held by device k of dp+region; they are its first rows; some device holds 32.
All inputs are finite; a program needn't handle non-finite values.
Results may differ from the reference program's by a relative error of at most 0.0025.
The reference program's roundings to bfloat16 on the way count: a program that leaves them out, or rounds other values in their place, can miss the bound.
Values may be sent and summed in bfloat16 or wider, within the bound.
No kernel may reach another device: no remote copies, remote signals or barrier semaphores. Data moves between devices by JAX's collectives and lax.ppermute only.
A program may use at most 64 MiB of HBM per device.

```python
import math
import jax
import jax.numpy as jnp
from jax import lax

BLOCK = 128
TILE_RAYS = 128
SLOTS = 8
ITERS = 2
TILES_DEV = 64
NB_DEV = 256
FACE_DEV = 32
TILES = 512
NB = 1024
FACES = 1024
N_DP = 8
N_REGION = 4


def draw_travel_times(key, part):
    key_base = jax.random.fold_in(key, 11)
    key_rows = jax.random.fold_in(key, 12)
    key_cols = jax.random.fold_in(key, 13)
    base_draw = jax.random.normal(key_base, (TILES, TILE_RAYS), jnp.float32)
    row_scale = jnp.exp(jax.random.uniform(key_rows, (TILES, 1), jnp.float32, 0.0, math.log(10.0)))
    base_draw = jnp.clip(base_draw, -6.0, 6.0)
    col_scale = jnp.exp(jax.random.uniform(key_cols, (1, TILE_RAYS), jnp.float32, 0.0, math.log(3.0)))
    rise_scale = 1.0 + 2.0 * jnp.arange(TILES).astype(jnp.float32)[:, None] / max(TILES - 1, 1)
    return (0.1 * base_draw * row_scale * col_scale * rise_scale).astype(jnp.float32)


def draw_face_blocks(key, part):
    key_first = jax.random.fold_in(key, 21)
    key_side = jax.random.fold_in(key, 22)
    key_second = jax.random.fold_in(key, 23)
    row_index = jnp.arange(FACES).astype(jnp.int32)
    owner_region = row_index // FACE_DEV % N_REGION
    first_block = owner_region * NB_DEV + jax.random.randint(key_first, (FACES,), 0, NB_DEV)
    which_side = jax.random.randint(key_side, (FACES,), 0, 8)
    offset = jnp.where(which_side < 4, 0, jnp.where(which_side < 5 + owner_region, 1, -1))
    other_region = (owner_region + offset + N_REGION) % N_REGION
    second_block = other_region * NB_DEV + jax.random.randint(key_second, (FACES,), 0, NB_DEV)
    return jnp.stack([first_block, second_block], axis=1).astype(jnp.int32)


def draw_face_count(key, part):
    key_counts = jax.random.fold_in(key, 31)
    key_full = jax.random.fold_in(key, 32)
    counts = jax.random.randint(key_counts, (N_DP * N_REGION,), FACE_DEV // 4, FACE_DEV + 1)
    full_index = jax.random.randint(key_full, (), 0, N_DP * N_REGION)
    device_index = jnp.arange(N_DP * N_REGION).astype(jnp.int32)
    return jnp.where(device_index == full_index, FACE_DEV, counts).astype(jnp.int32)


def touch_ends(entries, stream_key, low, top_value):
    place = [jax.random.randint(jax.random.fold_in(stream_key, axis), (), 0, length) for axis, length in enumerate(entries.shape)]
    main_axis = entries.shape.index(max(entries.shape))
    neighbour = place[:main_axis] + [(place[main_axis] + 1) % entries.shape[main_axis]] + place[main_axis + 1:]
    return entries.at[tuple(place)].set(low).at[tuple(neighbour)].set(top_value)


def block_scale(key, dims, cuts, smallest, largest):
    def one(dim, shards_of):
        steps = jax.random.uniform(jax.random.fold_in(jax.random.fold_in(key, 6), dim), (shards_of,), jnp.float32, smallest / len(cuts), largest / len(cuts))
        return jnp.repeat(jnp.exp(steps), dims[dim] // shards_of).reshape((-1,) + (1,) * (len(dims) - dim - 1))

    level = one(*cuts[0])
    for cut in cuts[1:]:
        level = level * one(*cut)
    return level


def scatter_about(own_key, extent, spread, bound, cuts=(), held_as=jnp.bfloat16):
    array = jax.random.normal(own_key, extent, jnp.float32) * spread
    if len(cuts) > 0:
        array = block_scale(own_key, extent, cuts, -0.22, 0.18) * array
    return jnp.clip(array, min=-bound, max=bound).astype(held_as)


def setup_inputs(seed: int = 0) -> dict:
    arg_keys = jax.random.split(jax.random.key(seed), 7)
    return {
        "travel_times": draw_travel_times(jax.random.fold_in(arg_keys[6], 71), 0),
        "sensitivity": scatter_about(arg_keys[1], (TILES, SLOTS, TILE_RAYS, BLOCK), (SLOTS * BLOCK) ** -0.5, 0.1875, ((0, 8), (1, 4))),
        "tile_blocks": touch_ends(jax.random.randint(arg_keys[2], (TILES, SLOTS), 0, NB), jax.random.fold_in(arg_keys[2], 1), 0, NB - 1).astype(jnp.int32),
        "face_blocks": draw_face_blocks(jax.random.fold_in(arg_keys[6], 71), 0),
        "face_weights": jnp.clip(jnp.exp(math.log(2.0) - 2.3025851 * jax.random.uniform(arg_keys[4], (FACES, BLOCK), jnp.float32) ** block_scale(arg_keys[4], (FACES, BLOCK), ((0, 32),), -0.2, 0.2)), 0.2, 2.0),
        "face_count": draw_face_count(jax.random.fold_in(arg_keys[6], 71), 0),
    }


smooth_weight = 1.0

def face_factors(face_weights, face_count):
    row_index = jnp.arange(FACES).astype(jnp.int32)
    owner_device = row_index // FACE_DEV
    live_mask = (row_index % FACE_DEV < face_count[owner_device]).astype(jnp.float32)
    return smooth_weight * face_weights * live_mask[:, None]

def ray_forward(sensitivity, tile_blocks, full_model):
    tile_sens = sensitivity.reshape(N_DP, TILES_DEV, SLOTS, TILE_RAYS, BLOCK)
    block_index = tile_blocks.reshape(N_DP, TILES_DEV, SLOTS)

    def one_block(tile_pair):
        sens_part, row_index = tile_pair
        picked = full_model[row_index].astype(jnp.float32)
        return jnp.einsum('tsrb,tsb->tr', sens_part.astype(jnp.float32), picked)
    return lax.map(one_block, (tile_sens, block_index)).reshape(TILES, TILE_RAYS)

def ray_transpose(sensitivity, tile_blocks, rays_half):
    tile_sens = sensitivity.reshape(N_DP, TILES_DEV, SLOTS, TILE_RAYS, BLOCK)
    block_index = tile_blocks.reshape(N_DP, TILES_DEV, SLOTS)
    ray_parts = rays_half.reshape(N_DP, TILES_DEV, TILE_RAYS)

    def accumulate(running, trio):
        sens_part, row_index, ray_part = trio
        contrib = jnp.einsum('tsrb,tr->tsb', sens_part.astype(jnp.float32), ray_part.astype(jnp.float32))
        added = jax.ops.segment_sum(contrib.reshape(-1, BLOCK), row_index.reshape(-1), num_segments=NB)
        return (running + added, None)
    running, _ = lax.scan(accumulate, jnp.zeros((NB, BLOCK), jnp.float32), (tile_sens, block_index, ray_parts))
    return running

def reference(travel_times, sensitivity, tile_blocks, face_blocks, face_weights, face_count):
    face_scale = face_factors(face_weights, face_count)
    first_block = face_blocks[:, 0]
    second_block = face_blocks[:, 1]

    def transposed(left_rays, left_faces):
        partials = ray_transpose(sensitivity, tile_blocks, left_rays.astype(jnp.bfloat16))
        face_term = face_scale * left_faces
        partials = partials + jax.ops.segment_sum(face_term, first_block, num_segments=NB)
        return partials - jax.ops.segment_sum(face_term, second_block, num_segments=NB)
    beta_value = jnp.sqrt(jnp.sum(travel_times * travel_times))
    left_rays = travel_times / beta_value
    left_faces = jnp.zeros((FACES, BLOCK), jnp.float32)
    right_vector = transposed(left_rays, left_faces)
    alpha_value = jnp.sqrt(jnp.sum(right_vector * right_vector))
    right_vector = right_vector / alpha_value
    direction = right_vector
    solution = jnp.zeros((NB, BLOCK), jnp.float32)
    phi_bar = beta_value
    rho_bar = alpha_value
    for iteration in range(ITERS):
        full_model = right_vector.astype(jnp.bfloat16)
        left_rays = ray_forward(sensitivity, tile_blocks, full_model) - alpha_value * left_rays
        face_term = face_scale * (full_model[first_block].astype(jnp.float32) - full_model[second_block].astype(jnp.float32))
        left_faces = face_term - alpha_value * left_faces
        beta_value = jnp.sqrt(jnp.sum(left_rays * left_rays) + jnp.sum(left_faces * left_faces))
        left_rays = left_rays / beta_value
        left_faces = left_faces / beta_value
        last_turn = iteration + 1 == ITERS
        if not last_turn:
            right_vector = transposed(left_rays, left_faces) - beta_value * right_vector
            alpha_new = jnp.sqrt(jnp.sum(right_vector * right_vector))
            right_vector = right_vector / alpha_new
        rho_value = jnp.sqrt(rho_bar * rho_bar + beta_value * beta_value)
        cosine = rho_bar / rho_value
        sine_value = beta_value / rho_value
        phi_value = cosine * phi_bar
        phi_bar = sine_value * phi_bar
        solution = solution + phi_value / rho_value * direction
        if not last_turn:
            rho_bar = -cosine * alpha_new
            direction = right_vector - sine_value * alpha_new / rho_value * direction
            alpha_value = alpha_new
    return solution
```

```python
import jax
import jax.numpy as jnp
from jax import lax
from jax.sharding import PartitionSpec as P

ITERS = 2
NB_DEV = 256


smooth_weight = 1.0


def butterfly_sum(x, axis):
    n = lax.axis_size(axis)
    if n & (n - 1):
        return lax.psum(x, axis)
    k = 1
    while k < n:
        x = x + lax.ppermute(x, axis, [(i, i ^ k) for i in range(n)])
        k *= 2
    return x


def halving_scatter(x, axis):
    n = lax.axis_size(axis)
    if n & (n - 1):
        summed = lax.psum(x, axis)
        rows = x.shape[0] // n
        return lax.dynamic_slice_in_dim(summed, lax.axis_index(axis) * rows, rows, 0)
    me = lax.axis_index(axis)
    k = n // 2
    while k >= 1:
        half = x.shape[0] // 2
        bit = (me // k) % 2
        keep = lax.dynamic_slice_in_dim(x, bit * half, half, 0)
        send = lax.dynamic_slice_in_dim(x, (1 - bit) * half, half, 0)
        x = keep + lax.ppermute(send, axis, [(i, i ^ k) for i in range(n)])
        k //= 2
    return x


def doubling_gather(x, axis):
    n = lax.axis_size(axis)
    if n & (n - 1):
        return lax.all_gather(x, axis, axis=0, tiled=True)
    me = lax.axis_index(axis)
    k = 1
    while k < n:
        other = lax.ppermute(x, axis, [(i, i ^ k) for i in range(n)])
        upper = (me // k) % 2 == 1
        x = jnp.where(upper, jnp.concatenate([other, x], 0), jnp.concatenate([x, other], 0))
        k *= 2
    return x


def local(travel_times, sensitivity, tile_blocks, face_blocks, face_weights, face_count):
    model_rows = NB_DEV * lax.axis_size("region")
    region = lax.axis_index("region")
    live_mask = (jnp.arange(face_blocks.shape[0]) < face_count[0]).astype(jnp.float32)
    face_scale = smooth_weight * face_weights * live_mask[:, None]
    first_block = face_blocks[:, 0]
    second_block = face_blocks[:, 1]
    flat_blocks = tile_blocks.reshape(-1)
    n_tiles = travel_times.shape[0]

    def transposed_part(left_rays, left_faces):
        rays_half = left_rays.astype(jnp.bfloat16)
        contrib = jnp.einsum(
            "tsrb,tr->tsb", sensitivity, rays_half, preferred_element_type=jnp.float32
        )
        contrib_rows = contrib.reshape(-1, contrib.shape[-1])
        face_term = face_scale * left_faces
        partials = jax.ops.segment_sum(contrib_rows, flat_blocks, num_segments=model_rows)
        partials = partials + jax.ops.segment_sum(face_term, first_block, num_segments=model_rows)
        partials = partials - jax.ops.segment_sum(face_term, second_block, num_segments=model_rows)
        piece = halving_scatter(partials, "region")
        return butterfly_sum(piece, "dp")

    def normalized_field(piece):
        field = doubling_gather(piece, "region")
        alpha = jnp.sqrt(jnp.sum(field * field))
        field = field / alpha
        return field, lax.dynamic_slice_in_dim(field, region * NB_DEV, NB_DEV, 0), alpha

    beta_value = jnp.sqrt(butterfly_sum(jnp.sum(travel_times * travel_times), "dp"))
    left_rays = travel_times / beta_value
    left_faces = jnp.zeros(face_weights.shape, jnp.float32)
    raw = transposed_part(left_rays, left_faces)
    full_model, right_vector, alpha_value = normalized_field(raw)
    direction = right_vector
    solution = jnp.zeros_like(right_vector)
    phi_bar = beta_value
    rho_bar = alpha_value
    for iteration in range(ITERS):
        full_half = full_model.astype(jnp.bfloat16)
        picked = full_half[tile_blocks]
        partial_value = jnp.einsum(
            "tsrb,tsb->tr", sensitivity, picked, preferred_element_type=jnp.float32
        )
        face_pred = face_scale * (
            full_half[first_block].astype(jnp.float32)
            - full_half[second_block].astype(jnp.float32)
        )
        left_faces = face_pred - alpha_value * left_faces
        face_sq = jnp.sum(left_faces * left_faces)
        packed = jnp.concatenate(
            [partial_value, jnp.broadcast_to(face_sq, (8, partial_value.shape[1]))], 0
        )
        packed = butterfly_sum(packed, "region")
        ray_pred = packed[:n_tiles]
        left_rays = ray_pred - alpha_value * left_rays
        beta_sq = butterfly_sum(jnp.sum(left_rays * left_rays) + packed[n_tiles, 0], "dp")
        beta_value = jnp.sqrt(beta_sq)
        left_rays = left_rays / beta_value
        left_faces = left_faces / beta_value
        last_turn = iteration + 1 == ITERS
        if not last_turn:
            raw = transposed_part(left_rays, left_faces) - beta_value * right_vector
            full_model, right_vector, alpha_new = normalized_field(raw)
        rho_value = jnp.sqrt(rho_bar * rho_bar + beta_value * beta_value)
        cosine = rho_bar / rho_value
        sine_value = beta_value / rho_value
        phi_value = cosine * phi_bar
        phi_bar = sine_value * phi_bar
        solution = solution + phi_value / rho_value * direction
        if not last_turn:
            rho_bar = -cosine * alpha_new
            direction = right_vector - sine_value * alpha_new / rho_value * direction
            alpha_value = alpha_new
    return solution


def solution(mesh):
    in_specs = (
        P("dp", None),
        P("dp", "region", None, None),
        P("dp", "region"),
        P(("dp", "region"), None),
        P(("dp", "region"), None),
        P(("dp", "region")),
    )
    out_specs = P("region", None)
    return jax.shard_map(local, mesh=mesh, in_specs=in_specs, out_specs=out_specs, check_vma=False)
```

```python
import jax
import jax.numpy as jnp
from jax import lax
from jax.sharding import PartitionSpec as P

ITERS = 2
NB_DEV = 256


smooth_weight = 1.0


def butterfly_sum(x, axis):
    n = lax.axis_size(axis)
    if n & (n - 1):
        return lax.psum(x, axis)
    k = 1
    while k < n:
        x = x + lax.ppermute(x, axis, [(i, i ^ k) for i in range(n)])
        k *= 2
    return x


def halving_scatter(x, axis):
    n = lax.axis_size(axis)
    if n & (n - 1):
        summed = lax.psum(x, axis)
        rows = x.shape[0] // n
        return lax.dynamic_slice_in_dim(summed, lax.axis_index(axis) * rows, rows, 0)
    me = lax.axis_index(axis)
    levels = n.bit_length() - 1
    x = x.reshape((2,) * levels + (x.shape[0] // n,) + x.shape[1:])
    k = 1
    while k < n:
        place = x.ndim - 3
        bit = (me // k) % 2
        keep = lax.dynamic_index_in_dim(x, bit, place, keepdims=False)
        send = lax.dynamic_index_in_dim(x, 1 - bit, place, keepdims=False)
        x = keep + lax.ppermute(send, axis, [(i, i ^ k) for i in range(n)])
        k *= 2
    return x


def doubling_gather(x, axis):
    n = lax.axis_size(axis)
    if n & (n - 1):
        return lax.all_gather(x, axis, axis=0, tiled=True)
    me = lax.axis_index(axis)
    rows = x.shape[0]
    k = n // 2
    while k >= 1:
        other = lax.ppermute(x, axis, [(i, i ^ k) for i in range(n)])
        upper = (me // k) % 2 == 1
        place = x.ndim - 2
        x = jnp.where(upper, jnp.stack([other, x], place), jnp.stack([x, other], place))
        k //= 2
    return x.reshape((n * rows,) + x.shape[-1:])


def local(travel_times, sensitivity, tile_blocks, face_blocks, face_weights, face_count):
    model_rows = NB_DEV * lax.axis_size("region")
    region = lax.axis_index("region")
    live_mask = (jnp.arange(face_blocks.shape[0]) < face_count[0]).astype(jnp.float32)
    face_scale = smooth_weight * face_weights * live_mask[:, None]
    first_block = face_blocks[:, 0]
    second_block = face_blocks[:, 1]
    flat_blocks = tile_blocks.reshape(-1)
    n_tiles = travel_times.shape[0]

    def transposed_part(left_rays, left_faces):
        rays_half = left_rays.astype(jnp.bfloat16)
        contrib = jnp.einsum(
            "tsrb,tr->tsb", sensitivity, rays_half, preferred_element_type=jnp.float32
        )
        contrib_rows = contrib.reshape(-1, contrib.shape[-1])
        face_term = face_scale * left_faces
        partials = jax.ops.segment_sum(contrib_rows, flat_blocks, num_segments=model_rows)
        partials = partials + jax.ops.segment_sum(face_term, first_block, num_segments=model_rows)
        partials = partials - jax.ops.segment_sum(face_term, second_block, num_segments=model_rows)
        piece = halving_scatter(partials, "region")
        return butterfly_sum(piece, "dp")

    def normalized_field(piece):
        field = doubling_gather(piece, "region")
        alpha = jnp.sqrt(jnp.sum(field * field))
        field = field / alpha
        return field, lax.dynamic_slice_in_dim(field, region * NB_DEV, NB_DEV, 0), alpha

    beta_value = jnp.sqrt(butterfly_sum(jnp.sum(travel_times * travel_times), "dp"))
    left_rays = travel_times / beta_value
    left_faces = jnp.zeros(face_weights.shape, jnp.float32)
    raw = transposed_part(left_rays, left_faces)
    full_model, right_vector, alpha_value = normalized_field(raw)
    direction = right_vector
    solution = jnp.zeros_like(right_vector)
    phi_bar = beta_value
    rho_bar = alpha_value
    for iteration in range(ITERS):
        full_half = full_model.astype(jnp.bfloat16)
        picked = full_half[tile_blocks]
        partial_value = jnp.einsum(
            "tsrb,tsb->tr", sensitivity, picked, preferred_element_type=jnp.float32
        )
        face_pred = face_scale * (
            full_half[first_block].astype(jnp.float32)
            - full_half[second_block].astype(jnp.float32)
        )
        left_faces = face_pred - alpha_value * left_faces
        face_sq = jnp.sum(left_faces * left_faces)
        packed = jnp.concatenate(
            [partial_value, jnp.broadcast_to(face_sq, (8, partial_value.shape[1]))], 0
        )
        packed = butterfly_sum(packed, "region")
        ray_pred = packed[:n_tiles]
        left_rays = ray_pred - alpha_value * left_rays
        beta_sq = butterfly_sum(jnp.sum(left_rays * left_rays) + packed[n_tiles, 0], "dp")
        beta_value = jnp.sqrt(beta_sq)
        left_rays = left_rays / beta_value
        left_faces = left_faces / beta_value
        last_turn = iteration + 1 == ITERS
        if not last_turn:
            raw = transposed_part(left_rays, left_faces) - beta_value * right_vector
            full_model, right_vector, alpha_new = normalized_field(raw)
        rho_value = jnp.sqrt(rho_bar * rho_bar + beta_value * beta_value)
        cosine = rho_bar / rho_value
        sine_value = beta_value / rho_value
        phi_value = cosine * phi_bar
        phi_bar = sine_value * phi_bar
        solution = solution + phi_value / rho_value * direction
        if not last_turn:
            rho_bar = -cosine * alpha_new
            direction = right_vector - sine_value * alpha_new / rho_value * direction
            alpha_value = alpha_new
    return solution


def solution(mesh):
    in_specs = (
        P("dp", None),
        P("dp", "region", None, None),
        P("dp", "region"),
        P(("dp", "region"), None),
        P(("dp", "region"), None),
        P(("dp", "region")),
    )
    out_specs = P("region", None)
    return jax.shard_map(local, mesh=mesh, in_specs=in_specs, out_specs=out_specs, check_vma=False)
```

```python
import jax
import jax.numpy as jnp
from jax import lax
from jax.sharding import PartitionSpec as P

ITERS = 2
NB_DEV = 256


smooth_weight = 1.0


def butterfly_sum(x, axis):
    n = lax.axis_size(axis)
    if n & (n - 1):
        return lax.psum(x, axis)
    k = 1
    while k < n:
        x = x + lax.ppermute(x, axis, [(i, i ^ k) for i in range(n)])
        k *= 2
    return x


def scalar_sum(value, axis):
    n = lax.axis_size(axis)
    spread = jnp.broadcast_to(value.astype(jnp.float32), (n, 1, 128))
    got = lax.all_to_all(spread, axis, 0, 0, tiled=False)
    total = got[0]
    for j in range(1, n):
        total = total + got[j]
    return total[0, 0]


def halving_scatter(x, axis):
    n = lax.axis_size(axis)
    if n & (n - 1):
        summed = lax.psum(x, axis)
        rows = x.shape[0] // n
        return lax.dynamic_slice_in_dim(summed, lax.axis_index(axis) * rows, rows, 0)
    me = lax.axis_index(axis)
    levels = n.bit_length() - 1
    x = x.reshape((2,) * levels + (x.shape[0] // n,) + x.shape[1:])
    k = 1
    while k < n:
        place = x.ndim - 3
        bit = (me // k) % 2
        keep = lax.dynamic_index_in_dim(x, bit, place, keepdims=False)
        send = lax.dynamic_index_in_dim(x, 1 - bit, place, keepdims=False)
        x = keep + lax.ppermute(send, axis, [(i, i ^ k) for i in range(n)])
        k *= 2
    return x


def doubling_gather(x, axis):
    n = lax.axis_size(axis)
    if n & (n - 1):
        return lax.all_gather(x, axis, axis=0, tiled=True)
    me = lax.axis_index(axis)
    rows = x.shape[0]
    k = n // 2
    while k >= 1:
        other = lax.ppermute(x, axis, [(i, i ^ k) for i in range(n)])
        upper = (me // k) % 2 == 1
        place = x.ndim - 2
        x = jnp.where(upper, jnp.stack([other, x], place), jnp.stack([x, other], place))
        k //= 2
    return x.reshape((n * rows,) + x.shape[-1:])


def local(travel_times, sensitivity, tile_blocks, face_blocks, face_weights, face_count):
    model_rows = NB_DEV * lax.axis_size("region")
    region = lax.axis_index("region")
    live_mask = (jnp.arange(face_blocks.shape[0]) < face_count[0]).astype(jnp.float32)
    face_scale = smooth_weight * face_weights * live_mask[:, None]
    first_block = face_blocks[:, 0]
    second_block = face_blocks[:, 1]
    flat_blocks = tile_blocks.reshape(-1)
    n_tiles = travel_times.shape[0]

    def transposed_part(left_rays, left_faces):
        rays_half = left_rays.astype(jnp.bfloat16)
        contrib = jnp.einsum(
            "tsrb,tr->tsb", sensitivity, rays_half, preferred_element_type=jnp.float32
        )
        contrib_rows = contrib.reshape(-1, contrib.shape[-1])
        face_term = face_scale * left_faces
        partials = jax.ops.segment_sum(contrib_rows, flat_blocks, num_segments=model_rows)
        partials = partials + jax.ops.segment_sum(face_term, first_block, num_segments=model_rows)
        partials = partials - jax.ops.segment_sum(face_term, second_block, num_segments=model_rows)
        piece = halving_scatter(partials, "region")
        return butterfly_sum(piece, "dp")

    def normalized_field(piece):
        field = doubling_gather(piece, "region")
        alpha = jnp.sqrt(jnp.sum(field * field))
        field = field / alpha
        return field, lax.dynamic_slice_in_dim(field, region * NB_DEV, NB_DEV, 0), alpha

    beta_value = jnp.sqrt(scalar_sum(jnp.sum(travel_times * travel_times), "dp"))
    left_rays = travel_times / beta_value
    left_faces = jnp.zeros(face_weights.shape, jnp.float32)
    raw = transposed_part(left_rays, left_faces)
    full_model, right_vector, alpha_value = normalized_field(raw)
    direction = right_vector
    solution = jnp.zeros_like(right_vector)
    phi_bar = beta_value
    rho_bar = alpha_value
    for iteration in range(ITERS):
        full_half = full_model.astype(jnp.bfloat16)
        picked = full_half[tile_blocks]
        partial_value = jnp.einsum(
            "tsrb,tsb->tr", sensitivity, picked, preferred_element_type=jnp.float32
        )
        face_pred = face_scale * (
            full_half[first_block].astype(jnp.float32)
            - full_half[second_block].astype(jnp.float32)
        )
        left_faces = face_pred - alpha_value * left_faces
        face_sq = jnp.sum(left_faces * left_faces)
        packed = jnp.concatenate(
            [partial_value, jnp.broadcast_to(face_sq, (8, partial_value.shape[1]))], 0
        )
        packed = butterfly_sum(packed, "region")
        ray_pred = packed[:n_tiles]
        left_rays = ray_pred - alpha_value * left_rays
        beta_sq = scalar_sum(jnp.sum(left_rays * left_rays) + packed[n_tiles, 0], "dp")
        beta_value = jnp.sqrt(beta_sq)
        left_rays = left_rays / beta_value
        left_faces = left_faces / beta_value
        last_turn = iteration + 1 == ITERS
        if not last_turn:
            raw = transposed_part(left_rays, left_faces) - beta_value * right_vector
            full_model, right_vector, alpha_new = normalized_field(raw)
        rho_value = jnp.sqrt(rho_bar * rho_bar + beta_value * beta_value)
        cosine = rho_bar / rho_value
        sine_value = beta_value / rho_value
        phi_value = cosine * phi_bar
        phi_bar = sine_value * phi_bar
        solution = solution + phi_value / rho_value * direction
        if not last_turn:
            rho_bar = -cosine * alpha_new
            direction = right_vector - sine_value * alpha_new / rho_value * direction
            alpha_value = alpha_new
    return solution


def solution(mesh):
    in_specs = (
        P("dp", None),
        P("dp", "region", None, None),
        P("dp", "region"),
        P(("dp", "region"), None),
        P(("dp", "region"), None),
        P(("dp", "region")),
    )
    out_specs = P("region", None)
    return jax.shard_map(local, mesh=mesh, in_specs=in_specs, out_specs=out_specs, check_vma=False)
```

```python
import jax
import jax.numpy as jnp
from jax import lax
from jax.sharding import PartitionSpec as P

ITERS = 2
NB_DEV = 256


smooth_weight = 1.0


def butterfly_sum(x, axis):
    n = lax.axis_size(axis)
    if n & (n - 1):
        return lax.psum(x, axis)
    k = 1
    while k < n:
        x = x + lax.ppermute(x, axis, [(i, i ^ k) for i in range(n)])
        k *= 2
    return x


def scalar_sum(value, axis):
    n = lax.axis_size(axis)
    spread = jnp.broadcast_to(value.astype(jnp.float32), (n, 1, 128))
    got = lax.all_to_all(spread, axis, 0, 0, tiled=False)
    total = got[0]
    for j in range(1, n):
        total = total + got[j]
    return total[0, 0]


def halving_scatter(x, axis):
    n = lax.axis_size(axis)
    if n & (n - 1):
        summed = lax.psum(x, axis)
        rows = x.shape[0] // n
        return lax.dynamic_slice_in_dim(summed, lax.axis_index(axis) * rows, rows, 0)
    me = lax.axis_index(axis)
    levels = n.bit_length() - 1
    x = x.reshape((2,) * levels + (x.shape[0] // n,) + x.shape[1:])
    k = 1
    while k < n:
        place = x.ndim - 3
        bit = (me // k) % 2
        keep = lax.dynamic_index_in_dim(x, bit, place, keepdims=False)
        send = lax.dynamic_index_in_dim(x, 1 - bit, place, keepdims=False)
        x = keep + lax.ppermute(send, axis, [(i, i ^ k) for i in range(n)])
        k *= 2
    return x


def doubling_gather(x, axis):
    n = lax.axis_size(axis)
    if n & (n - 1):
        return lax.all_gather(x, axis, axis=0, tiled=True)
    me = lax.axis_index(axis)
    rows = x.shape[0]
    k = n // 2
    while k >= 1:
        other = lax.ppermute(x, axis, [(i, i ^ k) for i in range(n)])
        upper = (me // k) % 2 == 1
        place = x.ndim - 2
        x = jnp.where(upper, jnp.stack([other, x], place), jnp.stack([x, other], place))
        k //= 2
    return x.reshape((n * rows,) + x.shape[-1:])


def local(travel_times, sensitivity, tile_blocks, face_blocks, face_weights, face_count):
    model_rows = NB_DEV * lax.axis_size("region")
    region = lax.axis_index("region")
    live_mask = (jnp.arange(face_blocks.shape[0]) < face_count[0]).astype(jnp.float32)
    face_scale = smooth_weight * face_weights * live_mask[:, None]
    first_block = face_blocks[:, 0]
    second_block = face_blocks[:, 1]
    flat_blocks = tile_blocks.reshape(-1)
    n_tiles = travel_times.shape[0]
    columns = jnp.arange(model_rows, dtype=jnp.int32)[None, :]
    select = jnp.concatenate(
        [
            (flat_blocks[:, None] == columns).astype(jnp.float32),
            (first_block[:, None] == columns).astype(jnp.float32)
            - (second_block[:, None] == columns).astype(jnp.float32),
        ],
        0,
    )
    select_half = select.astype(jnp.bfloat16)
    n_slots = flat_blocks.shape[0]

    def transposed_part(left_rays, left_faces):
        rays_half = left_rays.astype(jnp.bfloat16)
        contrib = jnp.einsum(
            "tsrb,tr->tsb", sensitivity, rays_half, preferred_element_type=jnp.float32
        )
        contrib_rows = contrib.reshape(-1, contrib.shape[-1])
        face_term = face_scale * left_faces
        partials = lax.dot_general(
            select,
            jnp.concatenate([contrib_rows, face_term], 0),
            (((0,), (0,)), ((), ())),
            precision=lax.Precision.HIGHEST,
            preferred_element_type=jnp.float32,
        )
        piece = halving_scatter(partials, "region")
        return butterfly_sum(piece, "dp")

    def normalized_field(piece):
        field = doubling_gather(piece, "region")
        alpha = jnp.sqrt(jnp.sum(field * field))
        field = field / alpha
        return field, lax.dynamic_slice_in_dim(field, region * NB_DEV, NB_DEV, 0), alpha

    beta_value = jnp.sqrt(scalar_sum(jnp.sum(travel_times * travel_times), "dp"))
    left_rays = travel_times / beta_value
    left_faces = jnp.zeros(face_weights.shape, jnp.float32)
    raw = transposed_part(left_rays, left_faces)
    full_model, right_vector, alpha_value = normalized_field(raw)
    direction = right_vector
    solution = jnp.zeros_like(right_vector)
    phi_bar = beta_value
    rho_bar = alpha_value
    for iteration in range(ITERS):
        full_half = full_model.astype(jnp.bfloat16)
        rows = jnp.dot(select_half, full_half, preferred_element_type=jnp.float32)
        picked = rows[:n_slots].astype(jnp.bfloat16).reshape(tile_blocks.shape + rows.shape[-1:])
        partial_value = jnp.einsum(
            "tsrb,tsb->tr", sensitivity, picked, preferred_element_type=jnp.float32
        )
        face_pred = face_scale * rows[n_slots:]
        left_faces = face_pred - alpha_value * left_faces
        face_sq = jnp.sum(left_faces * left_faces)
        packed = jnp.concatenate(
            [partial_value, jnp.broadcast_to(face_sq, (8, partial_value.shape[1]))], 0
        )
        packed = butterfly_sum(packed, "region")
        ray_pred = packed[:n_tiles]
        left_rays = ray_pred - alpha_value * left_rays
        beta_sq = scalar_sum(jnp.sum(left_rays * left_rays) + packed[n_tiles, 0], "dp")
        beta_value = jnp.sqrt(beta_sq)
        left_rays = left_rays / beta_value
        left_faces = left_faces / beta_value
        last_turn = iteration + 1 == ITERS
        if not last_turn:
            raw = transposed_part(left_rays, left_faces) - beta_value * right_vector
            full_model, right_vector, alpha_new = normalized_field(raw)
        rho_value = jnp.sqrt(rho_bar * rho_bar + beta_value * beta_value)
        cosine = rho_bar / rho_value
        sine_value = beta_value / rho_value
        phi_value = cosine * phi_bar
        phi_bar = sine_value * phi_bar
        solution = solution + phi_value / rho_value * direction
        if not last_turn:
            rho_bar = -cosine * alpha_new
            direction = right_vector - sine_value * alpha_new / rho_value * direction
            alpha_value = alpha_new
    return solution


def solution(mesh):
    in_specs = (
        P("dp", None),
        P("dp", "region", None, None),
        P("dp", "region"),
        P(("dp", "region"), None),
        P(("dp", "region"), None),
        P(("dp", "region")),
    )
    out_specs = P("region", None)
    return jax.shard_map(local, mesh=mesh, in_specs=in_specs, out_specs=out_specs, check_vma=False)
```

```python
import jax
import jax.numpy as jnp
from jax import lax
from jax.sharding import PartitionSpec as P

ITERS = 2
NB_DEV = 256


smooth_weight = 1.0


def butterfly_sum(x, axis):
    n = lax.axis_size(axis)
    if n & (n - 1):
        return lax.psum(x, axis)
    k = 1
    while k < n:
        x = x + lax.ppermute(x, axis, [(i, i ^ k) for i in range(n)])
        k *= 2
    return x


def scalar_sum(value, axis):
    n = lax.axis_size(axis)
    spread = jnp.broadcast_to(value.astype(jnp.float32), (n, 1, 128))
    got = lax.all_to_all(spread, axis, 0, 0, tiled=False)
    total = got[0]
    for j in range(1, n):
        total = total + got[j]
    return total[0, 0]


def halving_scatter(x, axis):
    n = lax.axis_size(axis)
    if n & (n - 1):
        summed = lax.psum(x, axis)
        rows = x.shape[0] // n
        return lax.dynamic_slice_in_dim(summed, lax.axis_index(axis) * rows, rows, 0)
    me = lax.axis_index(axis)
    levels = n.bit_length() - 1
    x = x.reshape((2,) * levels + (x.shape[0] // n,) + x.shape[1:])
    k = 1
    while k < n:
        place = x.ndim - 3
        bit = (me // k) % 2
        keep = lax.dynamic_index_in_dim(x, bit, place, keepdims=False)
        send = lax.dynamic_index_in_dim(x, 1 - bit, place, keepdims=False)
        x = keep + lax.ppermute(send, axis, [(i, i ^ k) for i in range(n)])
        k *= 2
    return x


def doubling_gather(x, axis):
    n = lax.axis_size(axis)
    if n & (n - 1):
        return lax.all_gather(x, axis, axis=0, tiled=True)
    me = lax.axis_index(axis)
    rows, trailing = x.shape[0], x.shape[1:]
    k = n // 2
    place = 0
    while k >= 1:
        other = lax.ppermute(x, axis, [(i, i ^ k) for i in range(n)])
        upper = (me // k) % 2 == 1
        x = jnp.where(upper, jnp.stack([other, x], place), jnp.stack([x, other], place))
        place += 1
        k //= 2
    return x.reshape((n * rows,) + trailing)


def local(travel_times, sensitivity, tile_blocks, face_blocks, face_weights, face_count):
    model_rows = NB_DEV * lax.axis_size("region")
    region = lax.axis_index("region")
    n_faces = face_blocks.shape[0]
    group_blocks = doubling_gather(face_blocks, "region")
    group_weights = doubling_gather(face_weights, "region")
    group_count = doubling_gather(face_count, "region")
    group_rows = jnp.arange(group_blocks.shape[0])
    group_live = (group_rows % n_faces < group_count[group_rows // n_faces]).astype(jnp.float32)
    group_scale = smooth_weight * group_weights * group_live[:, None]
    live_mask = (jnp.arange(n_faces) < face_count[0]).astype(jnp.float32)
    face_scale = smooth_weight * face_weights * live_mask[:, None]
    first_block = face_blocks[:, 0]
    second_block = face_blocks[:, 1]
    flat_blocks = tile_blocks.reshape(-1)
    n_tiles = travel_times.shape[0]
    n_slots = flat_blocks.shape[0]
    columns = jnp.arange(model_rows, dtype=jnp.int32)[None, :]

    def hits(blocks):
        return (blocks[:, None] == columns).astype(jnp.float32)

    own_select = jnp.concatenate(
        [hits(flat_blocks), hits(first_block) - hits(second_block)], 0
    )
    group_select = jnp.concatenate(
        [hits(flat_blocks), hits(group_blocks[:, 0]) - hits(group_blocks[:, 1])], 0
    ).astype(jnp.bfloat16)

    def transposed_part(left_rays, group_faces):
        rays_half = left_rays.astype(jnp.bfloat16)
        contrib = jnp.einsum(
            "tsrb,tr->tsb", sensitivity, rays_half, preferred_element_type=jnp.float32
        )
        contrib_rows = contrib.reshape(-1, contrib.shape[-1])
        left_faces = lax.dynamic_slice_in_dim(group_faces, region * n_faces, n_faces, 0)
        face_term = face_scale * left_faces
        partials = lax.dot_general(
            own_select,
            jnp.concatenate([contrib_rows, face_term], 0),
            (((0,), (0,)), ((), ())),
            precision=lax.Precision.HIGHEST,
            preferred_element_type=jnp.float32,
        )
        piece = halving_scatter(partials, "region")
        return butterfly_sum(piece, "dp")

    def normalized_field(piece):
        field = doubling_gather(piece, "region")
        alpha = jnp.sqrt(jnp.sum(field * field))
        field = field / alpha
        return field, lax.dynamic_slice_in_dim(field, region * NB_DEV, NB_DEV, 0), alpha

    beta_value = jnp.sqrt(scalar_sum(jnp.sum(travel_times * travel_times), "dp"))
    left_rays = travel_times / beta_value
    left_faces = jnp.zeros(group_weights.shape, jnp.float32)
    raw = transposed_part(left_rays, left_faces)
    full_model, right_vector, alpha_value = normalized_field(raw)
    direction = right_vector
    solution = jnp.zeros_like(right_vector)
    phi_bar = beta_value
    rho_bar = alpha_value
    for iteration in range(ITERS):
        full_half = full_model.astype(jnp.bfloat16)
        rows = jnp.dot(group_select, full_half, preferred_element_type=jnp.float32)
        picked = rows[:n_slots].astype(jnp.bfloat16).reshape(tile_blocks.shape + rows.shape[-1:])
        partial_value = jnp.einsum(
            "tsrb,tsb->tr", sensitivity, picked, preferred_element_type=jnp.float32
        )
        ray_pred = butterfly_sum(partial_value, "region")
        face_pred = group_scale * rows[n_slots:]
        left_faces = face_pred - alpha_value * left_faces
        face_sq = jnp.sum(left_faces * left_faces)
        left_rays = ray_pred - alpha_value * left_rays
        beta_sq = scalar_sum(jnp.sum(left_rays * left_rays) + face_sq, "dp")
        beta_value = jnp.sqrt(beta_sq)
        left_rays = left_rays / beta_value
        left_faces = left_faces / beta_value
        last_turn = iteration + 1 == ITERS
        if not last_turn:
            raw = transposed_part(left_rays, left_faces) - beta_value * right_vector
            full_model, right_vector, alpha_new = normalized_field(raw)
        rho_value = jnp.sqrt(rho_bar * rho_bar + beta_value * beta_value)
        cosine = rho_bar / rho_value
        sine_value = beta_value / rho_value
        phi_value = cosine * phi_bar
        phi_bar = sine_value * phi_bar
        solution = solution + phi_value / rho_value * direction
        if not last_turn:
            rho_bar = -cosine * alpha_new
            direction = right_vector - sine_value * alpha_new / rho_value * direction
            alpha_value = alpha_new
    return solution


def solution(mesh):
    in_specs = (
        P("dp", None),
        P("dp", "region", None, None),
        P("dp", "region"),
        P(("dp", "region"), None),
        P(("dp", "region"), None),
        P(("dp", "region")),
    )
    out_specs = P("region", None)
    return jax.shard_map(local, mesh=mesh, in_specs=in_specs, out_specs=out_specs, check_vma=False)
```

```python
import jax
import jax.numpy as jnp
from jax import lax
from jax.sharding import PartitionSpec as P

ITERS = 2
NB_DEV = 256


smooth_weight = 1.0


def butterfly_sum(x, axis):
    n = lax.axis_size(axis)
    if n & (n - 1):
        return lax.psum(x, axis)
    k = 1
    while k < n:
        x = x + lax.ppermute(x, axis, [(i, i ^ k) for i in range(n)])
        k *= 2
    return x


def scalar_sum(value, axis):
    n = lax.axis_size(axis)
    spread = jnp.broadcast_to(value.astype(jnp.float32), (n, 1, 128))
    got = lax.all_to_all(spread, axis, 0, 0, tiled=False)
    total = got[0]
    for j in range(1, n):
        total = total + got[j]
    return total[0, 0]


def halving_scatter(x, axis):
    n = lax.axis_size(axis)
    if n & (n - 1):
        summed = lax.psum(x, axis)
        rows = x.shape[0] // n
        return lax.dynamic_slice_in_dim(summed, lax.axis_index(axis) * rows, rows, 0)
    me = lax.axis_index(axis)
    levels = n.bit_length() - 1
    x = x.reshape((2,) * levels + (x.shape[0] // n,) + x.shape[1:])
    k = 1
    while k < n:
        place = x.ndim - 3
        bit = (me // k) % 2
        keep = lax.dynamic_index_in_dim(x, bit, place, keepdims=False)
        send = lax.dynamic_index_in_dim(x, 1 - bit, place, keepdims=False)
        x = keep + lax.ppermute(send, axis, [(i, i ^ k) for i in range(n)])
        k *= 2
    return x


def doubling_gather(x, axis):
    n = lax.axis_size(axis)
    if n & (n - 1):
        return lax.all_gather(x, axis, axis=0, tiled=True)
    me = lax.axis_index(axis)
    rows, trailing = x.shape[0], x.shape[1:]
    k = n // 2
    place = 0
    while k >= 1:
        other = lax.ppermute(x, axis, [(i, i ^ k) for i in range(n)])
        upper = (me // k) % 2 == 1
        x = jnp.where(upper, jnp.stack([other, x], place), jnp.stack([x, other], place))
        place += 1
        k //= 2
    return x.reshape((n * rows,) + trailing)


def local(travel_times, sensitivity, tile_blocks, face_blocks, face_weights, face_count):
    model_rows = NB_DEV * lax.axis_size("region")
    region = lax.axis_index("region")
    n_faces = face_blocks.shape[0]
    group_blocks = doubling_gather(face_blocks, "region")
    group_weights = doubling_gather(face_weights, "region")
    group_count = doubling_gather(face_count, "region")
    group_rows = jnp.arange(group_blocks.shape[0])
    group_live = (group_rows % n_faces < group_count[group_rows // n_faces]).astype(jnp.float32)
    group_scale = smooth_weight * group_weights * group_live[:, None]
    live_mask = (jnp.arange(n_faces) < face_count[0]).astype(jnp.float32)
    face_scale = smooth_weight * face_weights * live_mask[:, None]
    first_block = face_blocks[:, 0]
    second_block = face_blocks[:, 1]
    flat_blocks = tile_blocks.reshape(-1)
    n_tiles = travel_times.shape[0]
    n_slots = flat_blocks.shape[0]
    columns = jnp.arange(model_rows, dtype=jnp.int32)[None, :]

    def hits(blocks):
        return (blocks[:, None] == columns).astype(jnp.float32)

    own_select = jnp.concatenate(
        [hits(flat_blocks), hits(first_block) - hits(second_block)], 0
    )
    group_select = jnp.concatenate(
        [hits(flat_blocks), hits(group_blocks[:, 0]) - hits(group_blocks[:, 1])], 0
    ).astype(jnp.bfloat16)

    def transposed_part(left_rays, group_faces):
        rays_half = left_rays.astype(jnp.bfloat16)
        contrib = jnp.einsum(
            "tsrb,tr->tsb", sensitivity, rays_half, preferred_element_type=jnp.float32
        )
        contrib_rows = contrib.reshape(-1, contrib.shape[-1])
        left_faces = lax.dynamic_slice_in_dim(group_faces, region * n_faces, n_faces, 0)
        face_term = face_scale * left_faces
        partials = lax.dot_general(
            own_select,
            jnp.concatenate([contrib_rows, face_term], 0),
            (((0,), (0,)), ((), ())),
            precision=lax.Precision.HIGHEST,
            preferred_element_type=jnp.float32,
        )
        piece = halving_scatter(partials, "region")
        return butterfly_sum(piece, "dp")

    def normalized_field(piece):
        field = doubling_gather(piece, "region")
        alpha = jnp.sqrt(jnp.sum(field * field))
        field = field / alpha
        return field, lax.dynamic_slice_in_dim(field, region * NB_DEV, NB_DEV, 0), alpha

    beta_value = jnp.sqrt(scalar_sum(jnp.sum(travel_times * travel_times), "dp"))
    left_rays = travel_times / beta_value
    left_rays, group_select, group_scale = lax.optimization_barrier(
        (left_rays, group_select, group_scale)
    )
    left_faces = jnp.zeros(group_weights.shape, jnp.float32)
    raw = transposed_part(left_rays, left_faces)
    full_model, right_vector, alpha_value = normalized_field(raw)
    direction = right_vector
    solution = jnp.zeros_like(right_vector)
    phi_bar = beta_value
    rho_bar = alpha_value
    for iteration in range(ITERS):
        full_half = full_model.astype(jnp.bfloat16)
        rows = jnp.dot(group_select, full_half, preferred_element_type=jnp.float32)
        picked = rows[:n_slots].astype(jnp.bfloat16).reshape(tile_blocks.shape + rows.shape[-1:])
        partial_value = jnp.einsum(
            "tsrb,tsb->tr", sensitivity, picked, preferred_element_type=jnp.float32
        )
        ray_pred = butterfly_sum(partial_value, "region")
        face_pred = group_scale * rows[n_slots:]
        left_faces = face_pred - alpha_value * left_faces
        face_sq = jnp.sum(left_faces * left_faces)
        left_rays = ray_pred - alpha_value * left_rays
        beta_sq = scalar_sum(jnp.sum(left_rays * left_rays) + face_sq, "dp")
        beta_value = jnp.sqrt(beta_sq)
        left_rays = left_rays / beta_value
        left_faces = left_faces / beta_value
        last_turn = iteration + 1 == ITERS
        if not last_turn:
            raw = transposed_part(left_rays, left_faces) - beta_value * right_vector
            full_model, right_vector, alpha_new = normalized_field(raw)
        rho_value = jnp.sqrt(rho_bar * rho_bar + beta_value * beta_value)
        cosine = rho_bar / rho_value
        sine_value = beta_value / rho_value
        phi_value = cosine * phi_bar
        phi_bar = sine_value * phi_bar
        solution = solution + phi_value / rho_value * direction
        if not last_turn:
            rho_bar = -cosine * alpha_new
            direction = right_vector - sine_value * alpha_new / rho_value * direction
            alpha_value = alpha_new
    return solution


def solution(mesh):
    in_specs = (
        P("dp", None),
        P("dp", "region", None, None),
        P("dp", "region"),
        P(("dp", "region"), None),
        P(("dp", "region"), None),
        P(("dp", "region")),
    )
    out_specs = P("region", None)
    return jax.shard_map(local, mesh=mesh, in_specs=in_specs, out_specs=out_specs, check_vma=False)
```

```python
import jax
import jax.numpy as jnp
from jax import lax
from jax.sharding import PartitionSpec as P

ITERS = 2
NB_DEV = 256


smooth_weight = 1.0


def butterfly_sum(x, axis):
    n = lax.axis_size(axis)
    if n & (n - 1):
        return lax.psum(x, axis)
    k = 1
    while k < n:
        x = x + lax.ppermute(x, axis, [(i, i ^ k) for i in range(n)])
        k *= 2
    return x


def scalar_sum(value, axis):
    n = lax.psum(1, axis)
    spread = jnp.broadcast_to(value.astype(jnp.float32), (n, 1, 128))
    got = lax.all_to_all(spread, axis, 0, 0, tiled=False)
    total = got[0]
    for j in range(1, n):
        total = total + got[j]
    return total[0, 0]


def halving_scatter(x, axis):
    n = lax.axis_size(axis)
    if n & (n - 1):
        summed = lax.psum(x, axis)
        rows = x.shape[0] // n
        return lax.dynamic_slice_in_dim(summed, lax.axis_index(axis) * rows, rows, 0)
    me = lax.axis_index(axis)
    levels = n.bit_length() - 1
    x = x.reshape((2,) * levels + (x.shape[0] // n,) + x.shape[1:])
    k = 1
    while k < n:
        place = x.ndim - 3
        bit = (me // k) % 2
        keep = lax.dynamic_index_in_dim(x, bit, place, keepdims=False)
        send = lax.dynamic_index_in_dim(x, 1 - bit, place, keepdims=False)
        x = keep + lax.ppermute(send, axis, [(i, i ^ k) for i in range(n)])
        k *= 2
    return x


def doubling_gather(x, axis):
    n = lax.axis_size(axis)
    if n & (n - 1):
        return lax.all_gather(x, axis, axis=0, tiled=True)
    me = lax.axis_index(axis)
    rows = x.shape[0]
    k = n // 2
    while k >= 1:
        other = lax.ppermute(x, axis, [(i, i ^ k) for i in range(n)])
        upper = (me // k) % 2 == 1
        place = x.ndim - 2
        x = jnp.where(upper, jnp.stack([other, x], place), jnp.stack([x, other], place))
        k //= 2
    return x.reshape((n * rows,) + x.shape[-1:])


def local(travel_times, sensitivity, tile_blocks, face_blocks, face_weights, face_count):
    n_region = lax.axis_size("region")
    model_rows = NB_DEV * n_region
    region = lax.axis_index("region")
    live_mask = (jnp.arange(face_blocks.shape[0]) < face_count[0]).astype(jnp.float32)
    face_scale = smooth_weight * face_weights * live_mask[:, None]
    first_block = face_blocks[:, 0]
    second_block = face_blocks[:, 1]
    flat_blocks = tile_blocks.reshape(-1)
    n_tiles = travel_times.shape[0]
    columns = jnp.arange(model_rows, dtype=jnp.int32)[None, :]
    select = jnp.concatenate(
        [
            (flat_blocks[:, None] == columns).astype(jnp.float32),
            (first_block[:, None] == columns).astype(jnp.float32)
            - (second_block[:, None] == columns).astype(jnp.float32),
        ],
        0,
    )
    select_half = select.astype(jnp.bfloat16)
    n_slots = flat_blocks.shape[0]

    def transposed_part(left_rays, left_faces):
        rays_half = left_rays.astype(jnp.bfloat16)
        contrib = jnp.einsum(
            "tsrb,tr->tsb", sensitivity, rays_half, preferred_element_type=jnp.float32
        )
        contrib_rows = contrib.reshape(-1, contrib.shape[-1])
        face_term = face_scale * left_faces
        partials = lax.dot_general(
            select,
            jnp.concatenate([contrib_rows, face_term], 0),
            (((0,), (0,)), ((), ())),
            precision=lax.Precision.HIGHEST,
            preferred_element_type=jnp.float32,
        )
        piece = halving_scatter(partials, "region")
        return butterfly_sum(piece, "dp")

    def normalized_field(piece):
        field = doubling_gather(piece, "region")
        alpha = jnp.sqrt(jnp.sum(field * field))
        field = field / alpha
        return field, lax.dynamic_slice_in_dim(field, region * NB_DEV, NB_DEV, 0), alpha

    beta_value = jnp.sqrt(scalar_sum(jnp.sum(travel_times * travel_times), "dp"))
    left_rays = travel_times / beta_value
    left_faces = jnp.zeros(face_weights.shape, jnp.float32)
    raw = transposed_part(left_rays, left_faces)
    full_model, right_vector, alpha_value = normalized_field(raw)
    direction = right_vector
    solution = jnp.zeros_like(right_vector)
    phi_bar = beta_value
    rho_bar = alpha_value
    for iteration in range(ITERS):
        full_half = full_model.astype(jnp.bfloat16)
        rows = jnp.dot(select_half, full_half, preferred_element_type=jnp.float32)
        picked = rows[:n_slots].astype(jnp.bfloat16).reshape(tile_blocks.shape + rows.shape[-1:])
        partial_value = jnp.einsum(
            "tsrb,tsb->tr", sensitivity, picked, preferred_element_type=jnp.float32
        )
        ray_pred = butterfly_sum(partial_value, "region")
        face_pred = face_scale * rows[n_slots:]
        left_faces = face_pred - alpha_value * left_faces
        face_sq = jnp.sum(left_faces * left_faces)
        left_rays = ray_pred - alpha_value * left_rays
        if n_tiles % n_region == 0:
            share = n_tiles // n_region
            own_rays = lax.dynamic_slice_in_dim(left_rays, region * share, share, 0)
            ray_sq = jnp.sum(own_rays * own_rays)
        else:
            ray_sq = jnp.where(region == 0, jnp.sum(left_rays * left_rays), 0.0)
        beta_sq = scalar_sum(ray_sq + face_sq, ("dp", "region"))
        beta_value = jnp.sqrt(beta_sq)
        left_rays = left_rays / beta_value
        left_faces = left_faces / beta_value
        last_turn = iteration + 1 == ITERS
        if not last_turn:
            raw = transposed_part(left_rays, left_faces) - beta_value * right_vector
            full_model, right_vector, alpha_new = normalized_field(raw)
        rho_value = jnp.sqrt(rho_bar * rho_bar + beta_value * beta_value)
        cosine = rho_bar / rho_value
        sine_value = beta_value / rho_value
        phi_value = cosine * phi_bar
        phi_bar = sine_value * phi_bar
        solution = solution + phi_value / rho_value * direction
        if not last_turn:
            rho_bar = -cosine * alpha_new
            direction = right_vector - sine_value * alpha_new / rho_value * direction
            alpha_value = alpha_new
    return solution


def solution(mesh):
    in_specs = (
        P("dp", None),
        P("dp", "region", None, None),
        P("dp", "region"),
        P(("dp", "region"), None),
        P(("dp", "region"), None),
        P(("dp", "region")),
    )
    out_specs = P("region", None)
    return jax.shard_map(local, mesh=mesh, in_specs=in_specs, out_specs=out_specs, check_vma=False)
```

```python
import jax
import jax.numpy as jnp
from jax import lax
from jax.sharding import PartitionSpec as P

ITERS = 2
NB_DEV = 256


smooth_weight = 1.0


def butterfly_sum(x, axis):
    n = lax.axis_size(axis)
    if n & (n - 1):
        return lax.psum(x, axis)
    k = 1
    while k < n:
        x = x + lax.ppermute(x, axis, [(i, i ^ k) for i in range(n)])
        k *= 2
    return x


def scalar_sum(value, axis):
    n = lax.psum(1, axis)
    spread = jnp.broadcast_to(value.astype(jnp.float32), (n,))
    got = lax.all_to_all(spread, axis, 0, 0, tiled=True)
    return jnp.sum(got)


def halving_scatter(x, axis):
    n = lax.axis_size(axis)
    if n & (n - 1):
        summed = lax.psum(x, axis)
        rows = x.shape[0] // n
        return lax.dynamic_slice_in_dim(summed, lax.axis_index(axis) * rows, rows, 0)
    me = lax.axis_index(axis)
    levels = n.bit_length() - 1
    x = x.reshape((2,) * levels + (x.shape[0] // n,) + x.shape[1:])
    k = 1
    while k < n:
        place = x.ndim - 3
        bit = (me // k) % 2
        keep = lax.dynamic_index_in_dim(x, bit, place, keepdims=False)
        send = lax.dynamic_index_in_dim(x, 1 - bit, place, keepdims=False)
        x = keep + lax.ppermute(send, axis, [(i, i ^ k) for i in range(n)])
        k *= 2
    return x


def doubling_gather(x, axis):
    n = lax.axis_size(axis)
    if n & (n - 1):
        return lax.all_gather(x, axis, axis=0, tiled=True)
    me = lax.axis_index(axis)
    rows = x.shape[0]
    k = n // 2
    while k >= 1:
        other = lax.ppermute(x, axis, [(i, i ^ k) for i in range(n)])
        upper = (me // k) % 2 == 1
        place = x.ndim - 2
        x = jnp.where(upper, jnp.stack([other, x], place), jnp.stack([x, other], place))
        k //= 2
    return x.reshape((n * rows,) + x.shape[-1:])


def local(travel_times, sensitivity, tile_blocks, face_blocks, face_weights, face_count):
    n_region = lax.axis_size("region")
    model_rows = NB_DEV * n_region
    region = lax.axis_index("region")
    live_mask = (jnp.arange(face_blocks.shape[0]) < face_count[0]).astype(jnp.float32)
    face_scale = smooth_weight * face_weights * live_mask[:, None]
    first_block = face_blocks[:, 0]
    second_block = face_blocks[:, 1]
    flat_blocks = tile_blocks.reshape(-1)
    n_tiles = travel_times.shape[0]
    columns = jnp.arange(model_rows, dtype=jnp.int32)[None, :]
    select = jnp.concatenate(
        [
            (flat_blocks[:, None] == columns).astype(jnp.float32),
            (first_block[:, None] == columns).astype(jnp.float32)
            - (second_block[:, None] == columns).astype(jnp.float32),
        ],
        0,
    )
    select_half = select.astype(jnp.bfloat16)
    n_slots = flat_blocks.shape[0]

    def transposed_part(left_rays, left_faces):
        rays_half = left_rays.astype(jnp.bfloat16)
        contrib = jnp.einsum(
            "tsrb,tr->tsb", sensitivity, rays_half, preferred_element_type=jnp.float32
        )
        contrib_rows = contrib.reshape(-1, contrib.shape[-1])
        face_term = face_scale * left_faces
        partials = lax.dot_general(
            select,
            jnp.concatenate([contrib_rows, face_term], 0),
            (((0,), (0,)), ((), ())),
            precision=lax.Precision.HIGHEST,
            preferred_element_type=jnp.float32,
        )
        piece = halving_scatter(partials, "region")
        return butterfly_sum(piece, "dp")

    def normalized_field(piece):
        field = doubling_gather(piece, "region")
        alpha = jnp.sqrt(jnp.sum(field * field))
        field = field / alpha
        return field, lax.dynamic_slice_in_dim(field, region * NB_DEV, NB_DEV, 0), alpha

    beta_value = jnp.sqrt(scalar_sum(jnp.sum(travel_times * travel_times), "dp"))
    left_rays = travel_times / beta_value
    left_faces = jnp.zeros(face_weights.shape, jnp.float32)
    raw = transposed_part(left_rays, left_faces)
    full_model, right_vector, alpha_value = normalized_field(raw)
    direction = right_vector
    solution = jnp.zeros_like(right_vector)
    phi_bar = beta_value
    rho_bar = alpha_value
    for iteration in range(ITERS):
        full_half = full_model.astype(jnp.bfloat16)
        rows = jnp.dot(select_half, full_half, preferred_element_type=jnp.float32)
        picked = rows[:n_slots].astype(jnp.bfloat16).reshape(tile_blocks.shape + rows.shape[-1:])
        partial_value = jnp.einsum(
            "tsrb,tsb->tr", sensitivity, picked, preferred_element_type=jnp.float32
        )
        ray_pred = butterfly_sum(partial_value, "region")
        face_pred = face_scale * rows[n_slots:]
        left_faces = face_pred - alpha_value * left_faces
        face_sq = jnp.sum(left_faces * left_faces)
        left_rays = ray_pred - alpha_value * left_rays
        if n_tiles % n_region == 0:
            share = n_tiles // n_region
            own_rays = lax.dynamic_slice_in_dim(left_rays, region * share, share, 0)
            ray_sq = jnp.sum(own_rays * own_rays)
        else:
            ray_sq = jnp.where(region == 0, jnp.sum(left_rays * left_rays), 0.0)
        beta_sq = scalar_sum(ray_sq + face_sq, ("dp", "region"))
        beta_value = jnp.sqrt(beta_sq)
        left_rays = left_rays / beta_value
        left_faces = left_faces / beta_value
        last_turn = iteration + 1 == ITERS
        if not last_turn:
            raw = transposed_part(left_rays, left_faces) - beta_value * right_vector
            full_model, right_vector, alpha_new = normalized_field(raw)
        rho_value = jnp.sqrt(rho_bar * rho_bar + beta_value * beta_value)
        cosine = rho_bar / rho_value
        sine_value = beta_value / rho_value
        phi_value = cosine * phi_bar
        phi_bar = sine_value * phi_bar
        solution = solution + phi_value / rho_value * direction
        if not last_turn:
            rho_bar = -cosine * alpha_new
            direction = right_vector - sine_value * alpha_new / rho_value * direction
            alpha_value = alpha_new
    return solution


def solution(mesh):
    in_specs = (
        P("dp", None),
        P("dp", "region", None, None),
        P("dp", "region"),
        P(("dp", "region"), None),
        P(("dp", "region"), None),
        P(("dp", "region")),
    )
    out_specs = P("region", None)
    return jax.shard_map(local, mesh=mesh, in_specs=in_specs, out_specs=out_specs, check_vma=False)
```

```python
import jax
import jax.numpy as jnp
from jax import lax
from jax.sharding import PartitionSpec as P

ITERS = 2
NB_DEV = 256


smooth_weight = 1.0


def butterfly_sum(x, axis):
    n = lax.axis_size(axis)
    if n & (n - 1):
        return lax.psum(x, axis)
    k = 1
    while k < n:
        x = x + lax.ppermute(x, axis, [(i, i ^ k) for i in range(n)])
        k *= 2
    return x


def scalar_sum(value, axis):
    n = lax.psum(1, axis)
    spread = jnp.broadcast_to(value.astype(jnp.float32), (n, 1, 128))
    got = lax.all_to_all(spread, axis, 0, 0, tiled=False)
    total = got[0]
    for j in range(1, n):
        total = total + got[j]
    return total[0, 0]


def halving_scatter(x, axis):
    n = lax.axis_size(axis)
    if n & (n - 1):
        summed = lax.psum(x, axis)
        rows = x.shape[0] // n
        return lax.dynamic_slice_in_dim(summed, lax.axis_index(axis) * rows, rows, 0)
    me = lax.axis_index(axis)
    levels = n.bit_length() - 1
    x = x.reshape((2,) * levels + (x.shape[0] // n,) + x.shape[1:])
    k = 1
    while k < n:
        place = x.ndim - 3
        bit = (me // k) % 2
        keep = lax.dynamic_index_in_dim(x, bit, place, keepdims=False)
        send = lax.dynamic_index_in_dim(x, 1 - bit, place, keepdims=False)
        x = keep + lax.ppermute(send, axis, [(i, i ^ k) for i in range(n)])
        k *= 2
    return x


def doubling_gather(x, axis):
    n = lax.axis_size(axis)
    if n & (n - 1):
        return lax.all_gather(x, axis, axis=0, tiled=True)
    me = lax.axis_index(axis)
    rows = x.shape[0]
    k = n // 2
    while k >= 1:
        other = lax.ppermute(x, axis, [(i, i ^ k) for i in range(n)])
        upper = (me // k) % 2 == 1
        place = x.ndim - 2
        x = jnp.where(upper, jnp.stack([other, x], place), jnp.stack([x, other], place))
        k //= 2
    return x.reshape((n * rows,) + x.shape[-1:])


def local(travel_times, sensitivity, tile_blocks, face_blocks, face_weights, face_count):
    n_region = lax.axis_size("region")
    model_rows = NB_DEV * n_region
    region = lax.axis_index("region")
    live_mask = (jnp.arange(face_blocks.shape[0]) < face_count[0]).astype(jnp.float32)
    face_scale = smooth_weight * face_weights * live_mask[:, None]
    first_block = face_blocks[:, 0]
    second_block = face_blocks[:, 1]
    flat_blocks = tile_blocks.reshape(-1)
    n_tiles = travel_times.shape[0]
    columns = jnp.arange(model_rows, dtype=jnp.int32)[None, :]
    select = jnp.concatenate(
        [
            (flat_blocks[:, None] == columns).astype(jnp.float32),
            (first_block[:, None] == columns).astype(jnp.float32)
            - (second_block[:, None] == columns).astype(jnp.float32),
        ],
        0,
    )
    select_half = select.astype(jnp.bfloat16)
    select_triple = jnp.concatenate([select_half] * 3, 0)
    n_slots = flat_blocks.shape[0]

    def transposed_part(left_rays, left_faces):
        rays_half = left_rays.astype(jnp.bfloat16)
        contrib = jnp.einsum(
            "tsrb,tr->tsb", sensitivity, rays_half, preferred_element_type=jnp.float32
        )
        contrib_rows = contrib.reshape(-1, contrib.shape[-1])
        face_term = face_scale * left_faces
        terms = jnp.concatenate([contrib_rows, face_term], 0)
        high = terms.astype(jnp.bfloat16)
        rest = terms - high.astype(jnp.float32)
        middle = rest.astype(jnp.bfloat16)
        low = (rest - middle.astype(jnp.float32)).astype(jnp.bfloat16)
        partials = lax.dot_general(
            select_triple,
            jnp.concatenate([high, middle, low], 0),
            (((0,), (0,)), ((), ())),
            preferred_element_type=jnp.float32,
        )
        piece = halving_scatter(partials, "region")
        return butterfly_sum(piece, "dp")

    def normalized_field(piece):
        field = doubling_gather(piece, "region")
        alpha = jnp.sqrt(jnp.sum(field * field))
        field = field / alpha
        return field, lax.dynamic_slice_in_dim(field, region * NB_DEV, NB_DEV, 0), alpha

    beta_value = jnp.sqrt(scalar_sum(jnp.sum(travel_times * travel_times), "dp"))
    left_rays = travel_times / beta_value
    left_faces = jnp.zeros(face_weights.shape, jnp.float32)
    raw = transposed_part(left_rays, left_faces)
    full_model, right_vector, alpha_value = normalized_field(raw)
    direction = right_vector
    solution = jnp.zeros_like(right_vector)
    phi_bar = beta_value
    rho_bar = alpha_value
    for iteration in range(ITERS):
        full_half = full_model.astype(jnp.bfloat16)
        rows = jnp.dot(select_half, full_half, preferred_element_type=jnp.float32)
        picked = rows[:n_slots].astype(jnp.bfloat16).reshape(tile_blocks.shape + rows.shape[-1:])
        partial_value = jnp.einsum(
            "tsrb,tsb->tr", sensitivity, picked, preferred_element_type=jnp.float32
        )
        ray_pred = butterfly_sum(partial_value, "region")
        face_pred = face_scale * rows[n_slots:]
        left_faces = face_pred - alpha_value * left_faces
        face_sq = jnp.sum(left_faces * left_faces)
        left_rays = ray_pred - alpha_value * left_rays
        if n_tiles % n_region == 0:
            share = n_tiles // n_region
            own_rays = lax.dynamic_slice_in_dim(left_rays, region * share, share, 0)
            ray_sq = jnp.sum(own_rays * own_rays)
        else:
            ray_sq = jnp.where(region == 0, jnp.sum(left_rays * left_rays), 0.0)
        beta_sq = scalar_sum(ray_sq + face_sq, ("dp", "region"))
        beta_value = jnp.sqrt(beta_sq)
        left_rays = left_rays / beta_value
        left_faces = left_faces / beta_value
        last_turn = iteration + 1 == ITERS
        if not last_turn:
            raw = transposed_part(left_rays, left_faces) - beta_value * right_vector
            full_model, right_vector, alpha_new = normalized_field(raw)
        rho_value = jnp.sqrt(rho_bar * rho_bar + beta_value * beta_value)
        cosine = rho_bar / rho_value
        sine_value = beta_value / rho_value
        phi_value = cosine * phi_bar
        phi_bar = sine_value * phi_bar
        solution = solution + phi_value / rho_value * direction
        if not last_turn:
            rho_bar = -cosine * alpha_new
            direction = right_vector - sine_value * alpha_new / rho_value * direction
            alpha_value = alpha_new
    return solution


def solution(mesh):
    in_specs = (
        P("dp", None),
        P("dp", "region", None, None),
        P("dp", "region"),
        P(("dp", "region"), None),
        P(("dp", "region"), None),
        P(("dp", "region")),
    )
    out_specs = P("region", None)
    return jax.shard_map(local, mesh=mesh, in_specs=in_specs, out_specs=out_specs, check_vma=False)
```

```python
import jax
import jax.numpy as jnp
from jax import lax
from jax.sharding import PartitionSpec as P

ITERS = 2
NB_DEV = 256


smooth_weight = 1.0


def butterfly_sum(x, axis):
    n = lax.axis_size(axis)
    if n & (n - 1):
        return lax.psum(x, axis)
    k = 1
    while k < n:
        x = x + lax.ppermute(x, axis, [(i, i ^ k) for i in range(n)])
        k *= 2
    return x


def scalar_sum(value, axis):
    n = lax.psum(1, axis)
    spread = jnp.broadcast_to(value.astype(jnp.float32), (n, 1, 128))
    got = lax.all_to_all(spread, axis, 0, 0, tiled=False)
    total = got[0]
    for j in range(1, n):
        total = total + got[j]
    return total[0, 0]


def halving_scatter(x, axis):
    n = lax.axis_size(axis)
    if n & (n - 1):
        summed = lax.psum(x, axis)
        rows = x.shape[0] // n
        return lax.dynamic_slice_in_dim(summed, lax.axis_index(axis) * rows, rows, 0)
    me = lax.axis_index(axis)
    levels = n.bit_length() - 1
    x = x.reshape((2,) * levels + (x.shape[0] // n,) + x.shape[1:])
    k = 1
    while k < n:
        place = x.ndim - 3
        bit = (me // k) % 2
        keep = lax.dynamic_index_in_dim(x, bit, place, keepdims=False)
        send = lax.dynamic_index_in_dim(x, 1 - bit, place, keepdims=False)
        x = keep + lax.ppermute(send, axis, [(i, i ^ k) for i in range(n)])
        k *= 2
    return x


def doubling_gather(x, axis):
    n = lax.axis_size(axis)
    if n & (n - 1):
        return lax.all_gather(x, axis, axis=0, tiled=True)
    me = lax.axis_index(axis)
    rows = x.shape[0]
    k = n // 2
    while k >= 1:
        other = lax.ppermute(x, axis, [(i, i ^ k) for i in range(n)])
        upper = (me // k) % 2 == 1
        place = x.ndim - 2
        x = jnp.where(upper, jnp.stack([other, x], place), jnp.stack([x, other], place))
        k //= 2
    return x.reshape((n * rows,) + x.shape[-1:])


def local(travel_times, sensitivity, tile_blocks, face_blocks, face_weights, face_count):
    n_region = lax.axis_size("region")
    model_rows = NB_DEV * n_region
    region = lax.axis_index("region")
    live_mask = (jnp.arange(face_blocks.shape[0]) < face_count[0]).astype(jnp.float32)
    face_scale = smooth_weight * face_weights * live_mask[:, None]
    first_block = face_blocks[:, 0]
    second_block = face_blocks[:, 1]
    flat_blocks = tile_blocks.reshape(-1)
    n_tiles = travel_times.shape[0]
    columns = jnp.arange(model_rows, dtype=jnp.int32)[None, :]
    select = jnp.concatenate(
        [
            (flat_blocks[:, None] == columns).astype(jnp.float32),
            (first_block[:, None] == columns).astype(jnp.float32)
            - (second_block[:, None] == columns).astype(jnp.float32),
        ],
        0,
    )
    select_half = select.astype(jnp.bfloat16)
    select_triple = jnp.concatenate([select_half] * 3, 0)
    n_slots = flat_blocks.shape[0]

    def transposed_part(left_rays, left_faces):
        rays_half = left_rays.astype(jnp.bfloat16)
        contrib = jnp.einsum(
            "tsrb,tr->tsb", sensitivity, rays_half, preferred_element_type=jnp.float32
        )
        contrib_rows = contrib.reshape(-1, contrib.shape[-1])
        face_term = face_scale * left_faces
        terms = jnp.concatenate([contrib_rows, face_term], 0)
        high_wide = lax.reduce_precision(terms, exponent_bits=8, mantissa_bits=7)
        rest = terms - high_wide
        middle_wide = lax.reduce_precision(rest, exponent_bits=8, mantissa_bits=7)
        high = high_wide.astype(jnp.bfloat16)
        middle = middle_wide.astype(jnp.bfloat16)
        low = (rest - middle_wide).astype(jnp.bfloat16)
        partials = lax.dot_general(
            select_triple,
            jnp.concatenate([high, middle, low], 0),
            (((0,), (0,)), ((), ())),
            preferred_element_type=jnp.float32,
        )
        piece = halving_scatter(partials, "region")
        return butterfly_sum(piece, "dp")

    def normalized_field(piece):
        field = doubling_gather(piece, "region")
        alpha = jnp.sqrt(jnp.sum(field * field))
        field = field / alpha
        return field, lax.dynamic_slice_in_dim(field, region * NB_DEV, NB_DEV, 0), alpha

    beta_value = jnp.sqrt(scalar_sum(jnp.sum(travel_times * travel_times), "dp"))
    left_rays = travel_times / beta_value
    left_faces = jnp.zeros(face_weights.shape, jnp.float32)
    raw = transposed_part(left_rays, left_faces)
    full_model, right_vector, alpha_value = normalized_field(raw)
    direction = right_vector
    solution = jnp.zeros_like(right_vector)
    phi_bar = beta_value
    rho_bar = alpha_value
    for iteration in range(ITERS):
        full_half = full_model.astype(jnp.bfloat16)
        rows = jnp.dot(select_half, full_half, preferred_element_type=jnp.float32)
        picked = rows[:n_slots].astype(jnp.bfloat16).reshape(tile_blocks.shape + rows.shape[-1:])
        partial_value = jnp.einsum(
            "tsrb,tsb->tr", sensitivity, picked, preferred_element_type=jnp.float32
        )
        ray_pred = butterfly_sum(partial_value, "region")
        face_pred = face_scale * rows[n_slots:]
        left_faces = face_pred - alpha_value * left_faces
        face_sq = jnp.sum(left_faces * left_faces)
        left_rays = ray_pred - alpha_value * left_rays
        if n_tiles % n_region == 0:
            share = n_tiles // n_region
            own_rays = lax.dynamic_slice_in_dim(left_rays, region * share, share, 0)
            ray_sq = jnp.sum(own_rays * own_rays)
        else:
            ray_sq = jnp.where(region == 0, jnp.sum(left_rays * left_rays), 0.0)
        beta_sq = scalar_sum(ray_sq + face_sq, ("dp", "region"))
        beta_value = jnp.sqrt(beta_sq)
        left_rays = left_rays / beta_value
        left_faces = left_faces / beta_value
        last_turn = iteration + 1 == ITERS
        if not last_turn:
            raw = transposed_part(left_rays, left_faces) - beta_value * right_vector
            full_model, right_vector, alpha_new = normalized_field(raw)
        rho_value = jnp.sqrt(rho_bar * rho_bar + beta_value * beta_value)
        cosine = rho_bar / rho_value
        sine_value = beta_value / rho_value
        phi_value = cosine * phi_bar
        phi_bar = sine_value * phi_bar
        solution = solution + phi_value / rho_value * direction
        if not last_turn:
            rho_bar = -cosine * alpha_new
            direction = right_vector - sine_value * alpha_new / rho_value * direction
            alpha_value = alpha_new
    return solution


def solution(mesh):
    in_specs = (
        P("dp", None),
        P("dp", "region", None, None),
        P("dp", "region"),
        P(("dp", "region"), None),
        P(("dp", "region"), None),
        P(("dp", "region")),
    )
    out_specs = P("region", None)
    return jax.shard_map(local, mesh=mesh, in_specs=in_specs, out_specs=out_specs, check_vma=False)
```

```python
import jax
import jax.numpy as jnp
from jax import lax
from jax.sharding import PartitionSpec as P

ITERS = 2
NB_DEV = 256


smooth_weight = 1.0


def butterfly_sum(x, axis):
    n = lax.axis_size(axis)
    if n & (n - 1):
        return lax.psum(x, axis)
    k = 1
    while k < n:
        x = x + lax.ppermute(x, axis, [(i, i ^ k) for i in range(n)])
        k *= 2
    return x


def square_sum(rows, axis):
    n = lax.psum(1, axis)
    squares = rows * rows
    spread = jnp.dot(
        jnp.ones((n, squares.shape[0]), jnp.float32), squares, precision=lax.Precision.HIGHEST
    )
    got = lax.all_to_all(spread[:, None, :], axis, 0, 0, tiled=False)
    total = got[0]
    for j in range(1, n):
        total = total + got[j]
    return jnp.sum(total)


def halving_scatter(x, axis):
    n = lax.axis_size(axis)
    if n & (n - 1):
        summed = lax.psum(x, axis)
        rows = x.shape[0] // n
        return lax.dynamic_slice_in_dim(summed, lax.axis_index(axis) * rows, rows, 0)
    me = lax.axis_index(axis)
    levels = n.bit_length() - 1
    x = x.reshape((2,) * levels + (x.shape[0] // n,) + x.shape[1:])
    k = 1
    while k < n:
        place = x.ndim - 3
        bit = (me // k) % 2
        keep = lax.dynamic_index_in_dim(x, bit, place, keepdims=False)
        send = lax.dynamic_index_in_dim(x, 1 - bit, place, keepdims=False)
        x = keep + lax.ppermute(send, axis, [(i, i ^ k) for i in range(n)])
        k *= 2
    return x


def doubling_gather(x, axis):
    n = lax.axis_size(axis)
    if n & (n - 1):
        return lax.all_gather(x, axis, axis=0, tiled=True)
    me = lax.axis_index(axis)
    rows = x.shape[0]
    k = n // 2
    while k >= 1:
        other = lax.ppermute(x, axis, [(i, i ^ k) for i in range(n)])
        upper = (me // k) % 2 == 1
        place = x.ndim - 2
        x = jnp.where(upper, jnp.stack([other, x], place), jnp.stack([x, other], place))
        k //= 2
    return x.reshape((n * rows,) + x.shape[-1:])


def local(travel_times, sensitivity, tile_blocks, face_blocks, face_weights, face_count):
    n_region = lax.axis_size("region")
    model_rows = NB_DEV * n_region
    region = lax.axis_index("region")
    live_mask = (jnp.arange(face_blocks.shape[0]) < face_count[0]).astype(jnp.float32)
    face_scale = smooth_weight * face_weights * live_mask[:, None]
    first_block = face_blocks[:, 0]
    second_block = face_blocks[:, 1]
    flat_blocks = tile_blocks.reshape(-1)
    n_tiles = travel_times.shape[0]
    columns = jnp.arange(model_rows, dtype=jnp.int32)[None, :]
    select = jnp.concatenate(
        [
            (flat_blocks[:, None] == columns).astype(jnp.float32),
            (first_block[:, None] == columns).astype(jnp.float32)
            - (second_block[:, None] == columns).astype(jnp.float32),
        ],
        0,
    )
    select_half = select.astype(jnp.bfloat16)
    select_triple = jnp.concatenate([select_half] * 3, 0)
    n_slots = flat_blocks.shape[0]

    def transposed_part(left_rays, left_faces):
        rays_half = left_rays.astype(jnp.bfloat16)
        contrib = jnp.einsum(
            "tsrb,tr->tsb", sensitivity, rays_half, preferred_element_type=jnp.float32
        )
        contrib_rows = contrib.reshape(-1, contrib.shape[-1])
        face_term = face_scale * left_faces
        terms = jnp.concatenate([contrib_rows, face_term], 0)
        high_wide = lax.reduce_precision(terms, exponent_bits=8, mantissa_bits=7)
        rest = terms - high_wide
        middle_wide = lax.reduce_precision(rest, exponent_bits=8, mantissa_bits=7)
        high = high_wide.astype(jnp.bfloat16)
        middle = middle_wide.astype(jnp.bfloat16)
        low = (rest - middle_wide).astype(jnp.bfloat16)
        partials = lax.dot_general(
            select_triple,
            jnp.concatenate([high, middle, low], 0),
            (((0,), (0,)), ((), ())),
            preferred_element_type=jnp.float32,
        )
        piece = halving_scatter(partials, "region")
        return butterfly_sum(piece, "dp")

    def normalized_field(piece):
        field = doubling_gather(piece, "region")
        alpha = jnp.sqrt(jnp.sum(field * field))
        field = field / alpha
        return field, lax.dynamic_slice_in_dim(field, region * NB_DEV, NB_DEV, 0), alpha

    beta_value = jnp.sqrt(square_sum(travel_times, "dp"))
    left_rays = travel_times / beta_value
    left_faces = jnp.zeros(face_weights.shape, jnp.float32)
    raw = transposed_part(left_rays, left_faces)
    full_model, right_vector, alpha_value = normalized_field(raw)
    direction = right_vector
    solution = jnp.zeros_like(right_vector)
    phi_bar = beta_value
    rho_bar = alpha_value
    for iteration in range(ITERS):
        full_half = full_model.astype(jnp.bfloat16)
        rows = jnp.dot(select_half, full_half, preferred_element_type=jnp.float32)
        picked = rows[:n_slots].astype(jnp.bfloat16).reshape(tile_blocks.shape + rows.shape[-1:])
        partial_value = jnp.einsum(
            "tsrb,tsb->tr", sensitivity, picked, preferred_element_type=jnp.float32
        )
        ray_pred = butterfly_sum(partial_value, "region")
        face_pred = face_scale * rows[n_slots:]
        left_faces = face_pred - alpha_value * left_faces
        left_rays = ray_pred - alpha_value * left_rays
        if n_tiles % n_region == 0:
            share = n_tiles // n_region
            own_rays = lax.dynamic_slice_in_dim(left_rays, region * share, share, 0)
        else:
            own_rays = jnp.where(region == 0, left_rays, 0.0)
        beta_sq = square_sum(jnp.concatenate([own_rays, left_faces], 0), ("dp", "region"))
        beta_value = jnp.sqrt(beta_sq)
        left_rays = left_rays / beta_value
        left_faces = left_faces / beta_value
        last_turn = iteration + 1 == ITERS
        if not last_turn:
            raw = transposed_part(left_rays, left_faces) - beta_value * right_vector
            full_model, right_vector, alpha_new = normalized_field(raw)
        rho_value = jnp.sqrt(rho_bar * rho_bar + beta_value * beta_value)
        cosine = rho_bar / rho_value
        sine_value = beta_value / rho_value
        phi_value = cosine * phi_bar
        phi_bar = sine_value * phi_bar
        solution = solution + phi_value / rho_value * direction
        if not last_turn:
            rho_bar = -cosine * alpha_new
            direction = right_vector - sine_value * alpha_new / rho_value * direction
            alpha_value = alpha_new
    return solution


def solution(mesh):
    in_specs = (
        P("dp", None),
        P("dp", "region", None, None),
        P("dp", "region"),
        P(("dp", "region"), None),
        P(("dp", "region"), None),
        P(("dp", "region")),
    )
    out_specs = P("region", None)
    return jax.shard_map(local, mesh=mesh, in_specs=in_specs, out_specs=out_specs, check_vma=False)
```

```python
import jax
import jax.numpy as jnp
from jax import lax
from jax.sharding import PartitionSpec as P

ITERS = 2
NB_DEV = 256


smooth_weight = 1.0


def butterfly_sum(x, axis):
    n = lax.axis_size(axis)
    if n & (n - 1):
        return lax.psum(x, axis)
    k = 1
    while k < n:
        x = x + lax.ppermute(x, axis, [(i, i ^ k) for i in range(n)])
        k *= 2
    return x


def square_sum(rows, axis):
    n = lax.psum(1, axis)
    squares = rows * rows
    spread = jnp.dot(
        jnp.ones((n, squares.shape[0]), jnp.float32), squares, precision=lax.Precision.HIGHEST
    )
    got = lax.all_to_all(spread[:, None, :], axis, 0, 0, tiled=False)
    total = got[0]
    for j in range(1, n):
        total = total + got[j]
    return jnp.sum(total)


def halving_scatter(x, axis):
    n = lax.axis_size(axis)
    if n & (n - 1):
        summed = lax.psum(x, axis)
        rows = x.shape[0] // n
        return lax.dynamic_slice_in_dim(summed, lax.axis_index(axis) * rows, rows, 0)
    me = lax.axis_index(axis)
    levels = n.bit_length() - 1
    x = x.reshape((2,) * levels + (x.shape[0] // n,) + x.shape[1:])
    k = 1
    while k < n:
        place = x.ndim - 3
        bit = (me // k) % 2
        keep = lax.dynamic_index_in_dim(x, bit, place, keepdims=False)
        send = lax.dynamic_index_in_dim(x, 1 - bit, place, keepdims=False)
        x = keep + lax.ppermute(send, axis, [(i, i ^ k) for i in range(n)])
        k *= 2
    return x


def doubling_gather(x, axis):
    n = lax.axis_size(axis)
    if n & (n - 1):
        return lax.all_gather(x, axis, axis=0, tiled=True)
    me = lax.axis_index(axis)
    rows = x.shape[0]
    k = n // 2
    while k >= 1:
        other = lax.ppermute(x, axis, [(i, i ^ k) for i in range(n)])
        upper = (me // k) % 2 == 1
        place = x.ndim - 2
        x = jnp.where(upper, jnp.stack([other, x], place), jnp.stack([x, other], place))
        k //= 2
    return x.reshape((n * rows,) + x.shape[-1:])


def local(travel_times, sensitivity, tile_blocks, face_blocks, face_weights, face_count):
    n_region = lax.axis_size("region")
    model_rows = NB_DEV * n_region
    region = lax.axis_index("region")
    live_mask = (jnp.arange(face_blocks.shape[0]) < face_count[0]).astype(jnp.float32)
    face_scale = smooth_weight * face_weights * live_mask[:, None]
    first_block = face_blocks[:, 0]
    second_block = face_blocks[:, 1]
    flat_blocks = tile_blocks.reshape(-1)
    n_tiles = travel_times.shape[0]
    columns = jnp.arange(model_rows, dtype=jnp.int32)[None, :]
    select = jnp.concatenate(
        [
            (flat_blocks[:, None] == columns).astype(jnp.float32),
            (first_block[:, None] == columns).astype(jnp.float32)
            - (second_block[:, None] == columns).astype(jnp.float32),
        ],
        0,
    )
    select_half = select.astype(jnp.bfloat16)
    select_triple = jnp.concatenate([select_half] * 3, 0)
    n_slots = flat_blocks.shape[0]

    def transposed_part(left_rays, left_faces):
        rays_half = left_rays.astype(jnp.bfloat16)
        contrib = jnp.einsum(
            "tsrb,tr->tsb", sensitivity, rays_half, preferred_element_type=jnp.float32
        )
        contrib_rows = contrib.reshape(-1, contrib.shape[-1])
        face_term = face_scale * left_faces
        terms = jnp.concatenate([contrib_rows, face_term], 0)
        high_wide = lax.reduce_precision(terms, exponent_bits=8, mantissa_bits=7)
        rest = terms - high_wide
        middle_wide = lax.reduce_precision(rest, exponent_bits=8, mantissa_bits=7)
        high = high_wide.astype(jnp.bfloat16)
        middle = middle_wide.astype(jnp.bfloat16)
        low = (rest - middle_wide).astype(jnp.bfloat16)
        partials = lax.dot_general(
            select_triple,
            jnp.concatenate([high, middle, low], 0),
            (((0,), (0,)), ((), ())),
            preferred_element_type=jnp.float32,
        )
        piece = halving_scatter(partials, "region")
        return butterfly_sum(piece, "dp")

    def normalized_field(piece):
        field = doubling_gather(piece, "region")
        alpha = jnp.sqrt(jnp.sum(field * field))
        field = field / alpha
        return field, lax.dynamic_slice_in_dim(field, region * NB_DEV, NB_DEV, 0), alpha

    beta_value = jnp.sqrt(square_sum(travel_times, "dp"))
    left_rays = travel_times / beta_value
    left_faces = jnp.zeros(face_weights.shape, jnp.float32)
    raw = transposed_part(left_rays, left_faces)
    full_model, right_vector, alpha_value = normalized_field(raw)
    direction = right_vector
    solution = jnp.zeros_like(right_vector)
    phi_bar = beta_value
    rho_bar = alpha_value
    for iteration in range(ITERS):
        full_half = full_model.astype(jnp.bfloat16)
        rows = jnp.dot(select_half, full_half, preferred_element_type=jnp.float32)
        picked = rows[:n_slots].astype(jnp.bfloat16).reshape(tile_blocks.shape + rows.shape[-1:])
        half_tiles = n_tiles // 2 if n_tiles % 16 == 0 else n_tiles
        halves = []
        for lo in range(0, n_tiles, half_tiles):
            part = jnp.einsum(
                "tsrb,tsb->tr",
                sensitivity[lo:lo + half_tiles],
                picked[lo:lo + half_tiles],
                preferred_element_type=jnp.float32,
            )
            halves.append(butterfly_sum(part, "region"))
        ray_pred = jnp.concatenate(halves, 0) if len(halves) > 1 else halves[0]
        face_pred = face_scale * rows[n_slots:]
        left_faces = face_pred - alpha_value * left_faces
        left_rays = ray_pred - alpha_value * left_rays
        if n_tiles % n_region == 0:
            share = n_tiles // n_region
            own_rays = lax.dynamic_slice_in_dim(left_rays, region * share, share, 0)
        else:
            own_rays = jnp.where(region == 0, left_rays, 0.0)
        beta_sq = square_sum(jnp.concatenate([own_rays, left_faces], 0), ("dp", "region"))
        beta_value = jnp.sqrt(beta_sq)
        left_rays = left_rays / beta_value
        left_faces = left_faces / beta_value
        last_turn = iteration + 1 == ITERS
        if not last_turn:
            raw = transposed_part(left_rays, left_faces) - beta_value * right_vector
            full_model, right_vector, alpha_new = normalized_field(raw)
        rho_value = jnp.sqrt(rho_bar * rho_bar + beta_value * beta_value)
        cosine = rho_bar / rho_value
        sine_value = beta_value / rho_value
        phi_value = cosine * phi_bar
        phi_bar = sine_value * phi_bar
        solution = solution + phi_value / rho_value * direction
        if not last_turn:
            rho_bar = -cosine * alpha_new
            direction = right_vector - sine_value * alpha_new / rho_value * direction
            alpha_value = alpha_new
    return solution


def solution(mesh):
    in_specs = (
        P("dp", None),
        P("dp", "region", None, None),
        P("dp", "region"),
        P(("dp", "region"), None),
        P(("dp", "region"), None),
        P(("dp", "region")),
    )
    out_specs = P("region", None)
    return jax.shard_map(local, mesh=mesh, in_specs=in_specs, out_specs=out_specs, check_vma=False)
```

```python
import jax
import jax.numpy as jnp
from jax import lax
from jax.sharding import PartitionSpec as P

ITERS = 2
NB_DEV = 256


smooth_weight = 1.0


def butterfly_sum(x, axis):
    n = lax.axis_size(axis)
    if n & (n - 1):
        return lax.psum(x, axis)
    k = 1
    while k < n:
        x = x + lax.ppermute(x, axis, [(i, i ^ k) for i in range(n)])
        k *= 2
    return x


def butterfly_sum_split(x, axis, other):
    n, m = lax.axis_size(axis), lax.axis_size(other)
    if n & (n - 1) or m % 2:
        return butterfly_sum(x, axis)
    forward = [1 << j for j in range(n.bit_length() - 1)]
    orders = (forward, forward[::-1])
    for stage in range(len(forward)):
        perm = []
        for i in range(n):
            for j in range(m):
                k = orders[j % 2][stage]
                perm.append((i * m + j, (i ^ k) * m + j))
        x = x + lax.ppermute(x, (axis, other), perm)
    return x


def square_sum(rows, axis):
    n = lax.psum(1, axis)
    squares = rows * rows
    spread = jnp.dot(
        jnp.ones((n, squares.shape[0]), jnp.float32), squares, precision=lax.Precision.HIGHEST
    )
    got = lax.all_to_all(spread[:, None, :], axis, 0, 0, tiled=False)
    total = got[0]
    for j in range(1, n):
        total = total + got[j]
    return jnp.sum(total)


def halving_scatter(x, axis):
    n = lax.axis_size(axis)
    if n & (n - 1):
        summed = lax.psum(x, axis)
        rows = x.shape[0] // n
        return lax.dynamic_slice_in_dim(summed, lax.axis_index(axis) * rows, rows, 0)
    me = lax.axis_index(axis)
    levels = n.bit_length() - 1
    x = x.reshape((2,) * levels + (x.shape[0] // n,) + x.shape[1:])
    k = 1
    while k < n:
        place = x.ndim - 3
        bit = (me // k) % 2
        keep = lax.dynamic_index_in_dim(x, bit, place, keepdims=False)
        send = lax.dynamic_index_in_dim(x, 1 - bit, place, keepdims=False)
        x = keep + lax.ppermute(send, axis, [(i, i ^ k) for i in range(n)])
        k *= 2
    return x


def doubling_gather(x, axis):
    n = lax.axis_size(axis)
    if n & (n - 1):
        return lax.all_gather(x, axis, axis=0, tiled=True)
    me = lax.axis_index(axis)
    rows = x.shape[0]
    k = n // 2
    while k >= 1:
        other = lax.ppermute(x, axis, [(i, i ^ k) for i in range(n)])
        upper = (me // k) % 2 == 1
        place = x.ndim - 2
        x = jnp.where(upper, jnp.stack([other, x], place), jnp.stack([x, other], place))
        k //= 2
    return x.reshape((n * rows,) + x.shape[-1:])


def local(travel_times, sensitivity, tile_blocks, face_blocks, face_weights, face_count):
    n_region = lax.axis_size("region")
    model_rows = NB_DEV * n_region
    region = lax.axis_index("region")
    live_mask = (jnp.arange(face_blocks.shape[0]) < face_count[0]).astype(jnp.float32)
    face_scale = smooth_weight * face_weights * live_mask[:, None]
    first_block = face_blocks[:, 0]
    second_block = face_blocks[:, 1]
    flat_blocks = tile_blocks.reshape(-1)
    n_tiles = travel_times.shape[0]
    columns = jnp.arange(model_rows, dtype=jnp.int32)[None, :]
    select = jnp.concatenate(
        [
            (flat_blocks[:, None] == columns).astype(jnp.float32),
            (first_block[:, None] == columns).astype(jnp.float32)
            - (second_block[:, None] == columns).astype(jnp.float32),
        ],
        0,
    )
    select_half = select.astype(jnp.bfloat16)
    select_triple = jnp.concatenate([select_half] * 3, 0)
    n_slots = flat_blocks.shape[0]

    def transposed_part(left_rays, left_faces):
        rays_half = left_rays.astype(jnp.bfloat16)
        contrib = jnp.einsum(
            "tsrb,tr->tsb", sensitivity, rays_half, preferred_element_type=jnp.float32
        )
        contrib_rows = contrib.reshape(-1, contrib.shape[-1])
        face_term = face_scale * left_faces
        terms = jnp.concatenate([contrib_rows, face_term], 0)
        high_wide = lax.reduce_precision(terms, exponent_bits=8, mantissa_bits=7)
        rest = terms - high_wide
        middle_wide = lax.reduce_precision(rest, exponent_bits=8, mantissa_bits=7)
        high = high_wide.astype(jnp.bfloat16)
        middle = middle_wide.astype(jnp.bfloat16)
        low = (rest - middle_wide).astype(jnp.bfloat16)
        partials = lax.dot_general(
            select_triple,
            jnp.concatenate([high, middle, low], 0),
            (((0,), (0,)), ((), ())),
            preferred_element_type=jnp.float32,
        )
        piece = halving_scatter(partials, "region")
        return butterfly_sum_split(piece, "dp", "region")

    def normalized_field(piece):
        field = doubling_gather(piece, "region")
        alpha = jnp.sqrt(jnp.sum(field * field))
        field = field / alpha
        return field, lax.dynamic_slice_in_dim(field, region * NB_DEV, NB_DEV, 0), alpha

    beta_value = jnp.sqrt(square_sum(travel_times, "dp"))
    left_rays = travel_times / beta_value
    left_faces = jnp.zeros(face_weights.shape, jnp.float32)
    raw = transposed_part(left_rays, left_faces)
    full_model, right_vector, alpha_value = normalized_field(raw)
    direction = right_vector
    solution = jnp.zeros_like(right_vector)
    phi_bar = beta_value
    rho_bar = alpha_value
    for iteration in range(ITERS):
        full_half = full_model.astype(jnp.bfloat16)
        rows = jnp.dot(select_half, full_half, preferred_element_type=jnp.float32)
        picked = rows[:n_slots].astype(jnp.bfloat16).reshape(tile_blocks.shape + rows.shape[-1:])
        half_tiles = n_tiles // 2 if n_tiles % 16 == 0 else n_tiles
        halves = []
        for lo in range(0, n_tiles, half_tiles):
            part = jnp.einsum(
                "tsrb,tsb->tr",
                sensitivity[lo:lo + half_tiles],
                picked[lo:lo + half_tiles],
                preferred_element_type=jnp.float32,
            )
            halves.append(butterfly_sum(part, "region"))
        ray_pred = jnp.concatenate(halves, 0) if len(halves) > 1 else halves[0]
        face_pred = face_scale * rows[n_slots:]
        left_faces = face_pred - alpha_value * left_faces
        left_rays = ray_pred - alpha_value * left_rays
        if n_tiles % n_region == 0:
            share = n_tiles // n_region
            own_rays = lax.dynamic_slice_in_dim(left_rays, region * share, share, 0)
        else:
            own_rays = jnp.where(region == 0, left_rays, 0.0)
        beta_sq = square_sum(jnp.concatenate([own_rays, left_faces], 0), ("dp", "region"))
        beta_value = jnp.sqrt(beta_sq)
        left_rays = left_rays / beta_value
        left_faces = left_faces / beta_value
        last_turn = iteration + 1 == ITERS
        if not last_turn:
            raw = transposed_part(left_rays, left_faces) - beta_value * right_vector
            full_model, right_vector, alpha_new = normalized_field(raw)
        rho_value = jnp.sqrt(rho_bar * rho_bar + beta_value * beta_value)
        cosine = rho_bar / rho_value
        sine_value = beta_value / rho_value
        phi_value = cosine * phi_bar
        phi_bar = sine_value * phi_bar
        solution = solution + phi_value / rho_value * direction
        if not last_turn:
            rho_bar = -cosine * alpha_new
            direction = right_vector - sine_value * alpha_new / rho_value * direction
            alpha_value = alpha_new
    return solution


def solution(mesh):
    in_specs = (
        P("dp", None),
        P("dp", "region", None, None),
        P("dp", "region"),
        P(("dp", "region"), None),
        P(("dp", "region"), None),
        P(("dp", "region")),
    )
    out_specs = P("region", None)
    return jax.shard_map(local, mesh=mesh, in_specs=in_specs, out_specs=out_specs, check_vma=False)
```

```python
import jax
import jax.numpy as jnp
from jax import lax
from jax.sharding import PartitionSpec as P

ITERS = 2
NB_DEV = 256


smooth_weight = 1.0


def butterfly_sum(x, axis):
    n = lax.axis_size(axis)
    if n & (n - 1):
        return lax.psum(x, axis)
    k = 1
    while k < n:
        x = x + lax.ppermute(x, axis, [(i, i ^ k) for i in range(n)])
        k *= 2
    return x


def square_sum(rows, axis):
    n = lax.psum(1, axis)
    squares = rows * rows
    spread = jnp.dot(
        jnp.ones((n, squares.shape[0]), jnp.float32), squares, precision=lax.Precision.HIGHEST
    )
    got = lax.all_to_all(spread[:, None, :], axis, 0, 0, tiled=False)
    total = got[0]
    for j in range(1, n):
        total = total + got[j]
    return jnp.sum(total)


def halving_scatter(x, axis):
    n = lax.axis_size(axis)
    if n & (n - 1):
        summed = lax.psum(x, axis)
        rows = x.shape[0] // n
        return lax.dynamic_slice_in_dim(summed, lax.axis_index(axis) * rows, rows, 0)
    me = lax.axis_index(axis)
    levels = n.bit_length() - 1
    x = x.reshape((2,) * levels + (x.shape[0] // n,) + x.shape[1:])
    k = 1
    while k < n:
        place = x.ndim - 3
        bit = (me // k) % 2
        keep = lax.dynamic_index_in_dim(x, bit, place, keepdims=False)
        send = lax.dynamic_index_in_dim(x, 1 - bit, place, keepdims=False)
        x = keep + lax.ppermute(send, axis, [(i, i ^ k) for i in range(n)])
        k *= 2
    return x


def doubling_gather(x, axis):
    n = lax.axis_size(axis)
    if n & (n - 1):
        return lax.all_gather(x, axis, axis=0, tiled=True)
    me = lax.axis_index(axis)
    rows = x.shape[0]
    k = n // 2
    while k >= 1:
        other = lax.ppermute(x, axis, [(i, i ^ k) for i in range(n)])
        upper = (me // k) % 2 == 1
        place = x.ndim - 2
        x = jnp.where(upper, jnp.stack([other, x], place), jnp.stack([x, other], place))
        k //= 2
    return x.reshape((n * rows,) + x.shape[-1:])


def local(travel_times, sensitivity, tile_blocks, face_blocks, face_weights, face_count):
    n_region = lax.axis_size("region")
    model_rows = NB_DEV * n_region
    region = lax.axis_index("region")
    live_mask = (jnp.arange(face_blocks.shape[0]) < face_count[0]).astype(jnp.float32)
    face_scale = smooth_weight * face_weights * live_mask[:, None]
    first_block = face_blocks[:, 0]
    second_block = face_blocks[:, 1]
    flat_blocks = tile_blocks.reshape(-1)
    n_tiles = travel_times.shape[0]
    columns = jnp.arange(model_rows, dtype=jnp.int32)[None, :]
    select = jnp.concatenate(
        [
            (flat_blocks[:, None] == columns).astype(jnp.float32),
            (first_block[:, None] == columns).astype(jnp.float32)
            - (second_block[:, None] == columns).astype(jnp.float32),
        ],
        0,
    )
    select_half = select.astype(jnp.bfloat16)
    select_triple = jnp.concatenate([select_half] * 3, 0)
    n_slots = flat_blocks.shape[0]

    def transposed_part(left_rays, left_faces):
        rays_half = left_rays.astype(jnp.bfloat16)
        contrib = jnp.einsum(
            "tsrb,tr->tsb", sensitivity, rays_half, preferred_element_type=jnp.float32
        )
        contrib_rows = contrib.reshape(-1, contrib.shape[-1])
        face_term = face_scale * left_faces
        terms = jnp.concatenate([contrib_rows, face_term], 0)
        high_wide = lax.reduce_precision(terms, exponent_bits=8, mantissa_bits=7)
        rest = terms - high_wide
        middle_wide = lax.reduce_precision(rest, exponent_bits=8, mantissa_bits=7)
        high = high_wide.astype(jnp.bfloat16)
        middle = middle_wide.astype(jnp.bfloat16)
        low = (rest - middle_wide).astype(jnp.bfloat16)
        partials = lax.dot_general(
            select_triple,
            jnp.concatenate([high, middle, low], 0),
            (((0,), (0,)), ((), ())),
            preferred_element_type=jnp.float32,
        )
        piece = halving_scatter(partials, "region")
        return butterfly_sum(piece, "dp")

    def normalized_field(piece):
        field = doubling_gather(piece, "region")
        alpha = jnp.sqrt(jnp.sum(field * field))
        field = field / alpha
        return field, lax.dynamic_slice_in_dim(field, region * NB_DEV, NB_DEV, 0), alpha

    beta_value = jnp.sqrt(square_sum(travel_times, "dp"))
    left_rays = travel_times / beta_value
    left_faces = jnp.zeros(face_weights.shape, jnp.float32)
    raw = transposed_part(left_rays, left_faces)
    full_model, right_vector, alpha_value = normalized_field(raw)
    direction = right_vector
    solution = jnp.zeros_like(right_vector)
    phi_bar = beta_value
    rho_bar = alpha_value
    for iteration in range(ITERS):
        full_half = full_model.astype(jnp.bfloat16)
        rows = jnp.dot(select_half, full_half, preferred_element_type=jnp.float32)
        picked = rows[:n_slots].astype(jnp.bfloat16).reshape(tile_blocks.shape + rows.shape[-1:])
        half_tiles = n_tiles // 4 if n_tiles % 32 == 0 else n_tiles
        halves = []
        for lo in range(0, n_tiles, half_tiles):
            part = jnp.einsum(
                "tsrb,tsb->tr",
                sensitivity[lo:lo + half_tiles],
                picked[lo:lo + half_tiles],
                preferred_element_type=jnp.float32,
            )
            halves.append(butterfly_sum(part, "region"))
        ray_pred = jnp.concatenate(halves, 0) if len(halves) > 1 else halves[0]
        face_pred = face_scale * rows[n_slots:]
        left_faces = face_pred - alpha_value * left_faces
        left_rays = ray_pred - alpha_value * left_rays
        if n_tiles % n_region == 0:
            share = n_tiles // n_region
            own_rays = lax.dynamic_slice_in_dim(left_rays, region * share, share, 0)
        else:
            own_rays = jnp.where(region == 0, left_rays, 0.0)
        beta_sq = square_sum(jnp.concatenate([own_rays, left_faces], 0), ("dp", "region"))
        beta_value = jnp.sqrt(beta_sq)
        left_rays = left_rays / beta_value
        left_faces = left_faces / beta_value
        last_turn = iteration + 1 == ITERS
        if not last_turn:
            raw = transposed_part(left_rays, left_faces) - beta_value * right_vector
            full_model, right_vector, alpha_new = normalized_field(raw)
        rho_value = jnp.sqrt(rho_bar * rho_bar + beta_value * beta_value)
        cosine = rho_bar / rho_value
        sine_value = beta_value / rho_value
        phi_value = cosine * phi_bar
        phi_bar = sine_value * phi_bar
        solution = solution + phi_value / rho_value * direction
        if not last_turn:
            rho_bar = -cosine * alpha_new
            direction = right_vector - sine_value * alpha_new / rho_value * direction
            alpha_value = alpha_new
    return solution


def solution(mesh):
    in_specs = (
        P("dp", None),
        P("dp", "region", None, None),
        P("dp", "region"),
        P(("dp", "region"), None),
        P(("dp", "region"), None),
        P(("dp", "region")),
    )
    out_specs = P("region", None)
    return jax.shard_map(local, mesh=mesh, in_specs=in_specs, out_specs=out_specs, check_vma=False)
```

```python
import jax
import jax.numpy as jnp
from jax import lax
from jax.sharding import PartitionSpec as P

ITERS = 2
NB_DEV = 256


smooth_weight = 1.0


def butterfly_sum(x, axis):
    n = lax.axis_size(axis)
    if n & (n - 1):
        return lax.psum(x, axis)
    k = 1
    while k < n:
        x = x + lax.ppermute(x, axis, [(i, i ^ k) for i in range(n)])
        k *= 2
    return x


def square_sum(rows, axis):
    n = lax.psum(1, axis)
    squares = rows * rows
    high = lax.reduce_precision(squares, exponent_bits=8, mantissa_bits=7)
    rest = squares - high
    middle = lax.reduce_precision(rest, exponent_bits=8, mantissa_bits=7)
    parts = jnp.concatenate(
        [high.astype(jnp.bfloat16), middle.astype(jnp.bfloat16), (rest - middle).astype(jnp.bfloat16)], 0
    )
    spread = jnp.dot(
        jnp.ones((n, parts.shape[0]), jnp.bfloat16), parts, preferred_element_type=jnp.float32
    )
    got = lax.all_to_all(spread[:, None, :], axis, 0, 0, tiled=False)
    total = got[0]
    for j in range(1, n):
        total = total + got[j]
    return jnp.sum(total)


def halving_scatter(x, axis):
    n = lax.axis_size(axis)
    if n & (n - 1):
        summed = lax.psum(x, axis)
        rows = x.shape[0] // n
        return lax.dynamic_slice_in_dim(summed, lax.axis_index(axis) * rows, rows, 0)
    me = lax.axis_index(axis)
    levels = n.bit_length() - 1
    x = x.reshape((2,) * levels + (x.shape[0] // n,) + x.shape[1:])
    k = 1
    while k < n:
        place = x.ndim - 3
        bit = (me // k) % 2
        keep = lax.dynamic_index_in_dim(x, bit, place, keepdims=False)
        send = lax.dynamic_index_in_dim(x, 1 - bit, place, keepdims=False)
        x = keep + lax.ppermute(send, axis, [(i, i ^ k) for i in range(n)])
        k *= 2
    return x


def doubling_gather(x, axis):
    n = lax.axis_size(axis)
    if n & (n - 1):
        return lax.all_gather(x, axis, axis=0, tiled=True)
    me = lax.axis_index(axis)
    rows = x.shape[0]
    k = n // 2
    while k >= 1:
        other = lax.ppermute(x, axis, [(i, i ^ k) for i in range(n)])
        upper = (me // k) % 2 == 1
        place = x.ndim - 2
        x = jnp.where(upper, jnp.stack([other, x], place), jnp.stack([x, other], place))
        k //= 2
    return x.reshape((n * rows,) + x.shape[-1:])


def local(travel_times, sensitivity, tile_blocks, face_blocks, face_weights, face_count):
    n_region = lax.axis_size("region")
    model_rows = NB_DEV * n_region
    region = lax.axis_index("region")
    live_mask = (jnp.arange(face_blocks.shape[0]) < face_count[0]).astype(jnp.float32)
    face_scale = smooth_weight * face_weights * live_mask[:, None]
    first_block = face_blocks[:, 0]
    second_block = face_blocks[:, 1]
    flat_blocks = tile_blocks.reshape(-1)
    n_tiles = travel_times.shape[0]
    columns = jnp.arange(model_rows, dtype=jnp.int32)[None, :]
    select = jnp.concatenate(
        [
            (flat_blocks[:, None] == columns).astype(jnp.float32),
            (first_block[:, None] == columns).astype(jnp.float32)
            - (second_block[:, None] == columns).astype(jnp.float32),
        ],
        0,
    )
    select_half = select.astype(jnp.bfloat16)
    select_triple = jnp.concatenate([select_half] * 3, 0)
    n_slots = flat_blocks.shape[0]

    def transposed_part(left_rays, left_faces):
        rays_half = left_rays.astype(jnp.bfloat16)
        contrib = jnp.einsum(
            "tsrb,tr->tsb", sensitivity, rays_half, preferred_element_type=jnp.float32
        )
        contrib_rows = contrib.reshape(-1, contrib.shape[-1])
        face_term = face_scale * left_faces
        terms = jnp.concatenate([contrib_rows, face_term], 0)
        high_wide = lax.reduce_precision(terms, exponent_bits=8, mantissa_bits=7)
        rest = terms - high_wide
        middle_wide = lax.reduce_precision(rest, exponent_bits=8, mantissa_bits=7)
        high = high_wide.astype(jnp.bfloat16)
        middle = middle_wide.astype(jnp.bfloat16)
        low = (rest - middle_wide).astype(jnp.bfloat16)
        partials = lax.dot_general(
            select_triple,
            jnp.concatenate([high, middle, low], 0),
            (((0,), (0,)), ((), ())),
            preferred_element_type=jnp.float32,
        )
        piece = halving_scatter(partials, "region")
        return butterfly_sum(piece, "dp")

    def normalized_field(piece):
        field = doubling_gather(piece, "region")
        alpha = jnp.sqrt(jnp.sum(field * field))
        field = field / alpha
        return field, lax.dynamic_slice_in_dim(field, region * NB_DEV, NB_DEV, 0), alpha

    beta_value = jnp.sqrt(square_sum(travel_times, "dp"))
    left_rays = travel_times / beta_value
    left_faces = jnp.zeros(face_weights.shape, jnp.float32)
    raw = transposed_part(left_rays, left_faces)
    full_model, right_vector, alpha_value = normalized_field(raw)
    direction = right_vector
    solution = jnp.zeros_like(right_vector)
    phi_bar = beta_value
    rho_bar = alpha_value
    for iteration in range(ITERS):
        full_half = full_model.astype(jnp.bfloat16)
        rows = jnp.dot(select_half, full_half, preferred_element_type=jnp.float32)
        picked = rows[:n_slots].astype(jnp.bfloat16).reshape(tile_blocks.shape + rows.shape[-1:])
        half_tiles = n_tiles // 2 if n_tiles % 16 == 0 else n_tiles
        halves = []
        for lo in range(0, n_tiles, half_tiles):
            part = jnp.einsum(
                "tsrb,tsb->tr",
                sensitivity[lo:lo + half_tiles],
                picked[lo:lo + half_tiles],
                preferred_element_type=jnp.float32,
            )
            halves.append(butterfly_sum(part, "region"))
        ray_pred = jnp.concatenate(halves, 0) if len(halves) > 1 else halves[0]
        face_pred = face_scale * rows[n_slots:]
        left_faces = face_pred - alpha_value * left_faces
        left_rays = ray_pred - alpha_value * left_rays
        if n_tiles % n_region == 0:
            share = n_tiles // n_region
            own_rays = lax.dynamic_slice_in_dim(left_rays, region * share, share, 0)
        else:
            own_rays = jnp.where(region == 0, left_rays, 0.0)
        beta_sq = square_sum(jnp.concatenate([own_rays, left_faces], 0), ("dp", "region"))
        beta_value = jnp.sqrt(beta_sq)
        left_rays = left_rays / beta_value
        left_faces = left_faces / beta_value
        last_turn = iteration + 1 == ITERS
        if not last_turn:
            raw = transposed_part(left_rays, left_faces) - beta_value * right_vector
            full_model, right_vector, alpha_new = normalized_field(raw)
        rho_value = jnp.sqrt(rho_bar * rho_bar + beta_value * beta_value)
        cosine = rho_bar / rho_value
        sine_value = beta_value / rho_value
        phi_value = cosine * phi_bar
        phi_bar = sine_value * phi_bar
        solution = solution + phi_value / rho_value * direction
        if not last_turn:
            rho_bar = -cosine * alpha_new
            direction = right_vector - sine_value * alpha_new / rho_value * direction
            alpha_value = alpha_new
    return solution


def solution(mesh):
    in_specs = (
        P("dp", None),
        P("dp", "region", None, None),
        P("dp", "region"),
        P(("dp", "region"), None),
        P(("dp", "region"), None),
        P(("dp", "region")),
    )
    out_specs = P("region", None)
    return jax.shard_map(local, mesh=mesh, in_specs=in_specs, out_specs=out_specs, check_vma=False)
```

```python
import jax
import jax.numpy as jnp
from jax import lax
from jax.sharding import PartitionSpec as P

ITERS = 2
NB_DEV = 256


smooth_weight = 1.0


def butterfly_sum(x, axis):
    n = lax.axis_size(axis)
    if n & (n - 1):
        return lax.psum(x, axis)
    k = 1
    while k < n:
        x = x + lax.ppermute(x, axis, [(i, i ^ k) for i in range(n)])
        k *= 2
    return x


def square_sum(rows, axis):
    n = lax.psum(1, axis)
    squares = rows * rows
    spread = jnp.dot(
        jnp.ones((n, squares.shape[0]), jnp.float32), squares, precision=lax.Precision.HIGHEST
    )
    got = lax.all_to_all(spread[:, None, :], axis, 0, 0, tiled=False)
    total = got[0]
    for j in range(1, n):
        total = total + got[j]
    return jnp.sum(total)


def halving_scatter(x, axis):
    n = lax.axis_size(axis)
    if n & (n - 1):
        summed = lax.psum(x, axis)
        rows = x.shape[0] // n
        return lax.dynamic_slice_in_dim(summed, lax.axis_index(axis) * rows, rows, 0)
    me = lax.axis_index(axis)
    levels = n.bit_length() - 1
    x = x.reshape((2,) * levels + (x.shape[0] // n,) + x.shape[1:])
    k = 1
    while k < n:
        place = x.ndim - 3
        bit = (me // k) % 2
        keep = lax.dynamic_index_in_dim(x, bit, place, keepdims=False)
        send = lax.dynamic_index_in_dim(x, 1 - bit, place, keepdims=False)
        x = keep + lax.ppermute(send, axis, [(i, i ^ k) for i in range(n)])
        k *= 2
    return x


def doubling_gather(x, axis):
    n = lax.axis_size(axis)
    if n & (n - 1):
        return lax.all_gather(x, axis, axis=0, tiled=True)
    me = lax.axis_index(axis)
    rows = x.shape[0]
    k = n // 2
    while k >= 1:
        other = lax.ppermute(x, axis, [(i, i ^ k) for i in range(n)])
        upper = (me // k) % 2 == 1
        place = x.ndim - 2
        x = jnp.where(upper, jnp.stack([other, x], place), jnp.stack([x, other], place))
        k //= 2
    return x.reshape((n * rows,) + x.shape[-1:])


def local(travel_times, sensitivity, tile_blocks, face_blocks, face_weights, face_count):
    n_region = lax.axis_size("region")
    model_rows = NB_DEV * n_region
    region = lax.axis_index("region")
    live_mask = (jnp.arange(face_blocks.shape[0]) < face_count[0]).astype(jnp.float32)
    face_scale = smooth_weight * face_weights * live_mask[:, None]
    first_block = face_blocks[:, 0]
    second_block = face_blocks[:, 1]
    flat_blocks = tile_blocks.reshape(-1)
    n_tiles = travel_times.shape[0]
    columns = jnp.arange(model_rows, dtype=jnp.int32)[None, :]
    select = jnp.concatenate(
        [
            (flat_blocks[:, None] == columns).astype(jnp.float32),
            (first_block[:, None] == columns).astype(jnp.float32)
            - (second_block[:, None] == columns).astype(jnp.float32),
        ],
        0,
    )
    select_half = select.astype(jnp.bfloat16)
    select_triple = jnp.concatenate([select_half] * 3, 0)
    n_slots = flat_blocks.shape[0]

    def transposed_part(left_rays, left_faces):
        rays_half = left_rays.astype(jnp.bfloat16)
        contrib = jnp.einsum(
            "tsrb,tr->tsb", sensitivity, rays_half, preferred_element_type=jnp.float32
        )
        contrib_rows = contrib.reshape(-1, contrib.shape[-1])
        face_term = face_scale * left_faces
        terms = jnp.concatenate([contrib_rows, face_term], 0)
        high_wide = lax.reduce_precision(terms, exponent_bits=8, mantissa_bits=7)
        rest = terms - high_wide
        middle_wide = lax.reduce_precision(rest, exponent_bits=8, mantissa_bits=7)
        high = high_wide.astype(jnp.bfloat16)
        middle = middle_wide.astype(jnp.bfloat16)
        low = (rest - middle_wide).astype(jnp.bfloat16)
        partials = lax.dot_general(
            select_triple,
            jnp.concatenate([high, middle, low], 0),
            (((0,), (0,)), ((), ())),
            preferred_element_type=jnp.float32,
        )
        piece = halving_scatter(partials, "region")
        return butterfly_sum(piece, "dp")

    def normalized_field(piece):
        field = doubling_gather(piece, "region")
        alpha = jnp.sqrt(jnp.sum(field * field))
        field = field / alpha
        return field, lax.dynamic_slice_in_dim(field, region * NB_DEV, NB_DEV, 0), alpha

    beta_value = jnp.sqrt(square_sum(travel_times, "dp"))
    left_rays = travel_times / beta_value
    left_faces = jnp.zeros(face_weights.shape, jnp.float32)
    raw = transposed_part(left_rays, left_faces)
    full_model, right_vector, alpha_value = normalized_field(raw)
    direction = right_vector
    solution = jnp.zeros_like(right_vector)
    phi_bar = beta_value
    rho_bar = alpha_value
    for iteration in range(ITERS):
        full_half = full_model.astype(jnp.bfloat16)
        rows = jnp.dot(select_half, full_half, preferred_element_type=jnp.float32)
        picked = rows[:n_slots].astype(jnp.bfloat16).reshape(tile_blocks.shape + rows.shape[-1:])
        cut = 3 * n_tiles // 4 if n_tiles % 32 == 0 else n_tiles
        halves = []
        for lo, hi in ((0, cut), (cut, n_tiles)):
            if hi == lo:
                continue
            part = jnp.einsum(
                "tsrb,tsb->tr",
                sensitivity[lo:hi],
                picked[lo:hi],
                preferred_element_type=jnp.float32,
            )
            halves.append(butterfly_sum(part, "region"))
        ray_pred = jnp.concatenate(halves, 0) if len(halves) > 1 else halves[0]
        face_pred = face_scale * rows[n_slots:]
        left_faces = face_pred - alpha_value * left_faces
        left_rays = ray_pred - alpha_value * left_rays
        if n_tiles % n_region == 0:
            share = n_tiles // n_region
            own_rays = lax.dynamic_slice_in_dim(left_rays, region * share, share, 0)
        else:
            own_rays = jnp.where(region == 0, left_rays, 0.0)
        beta_sq = square_sum(jnp.concatenate([own_rays, left_faces], 0), ("dp", "region"))
        beta_value = jnp.sqrt(beta_sq)
        left_rays = left_rays / beta_value
        left_faces = left_faces / beta_value
        last_turn = iteration + 1 == ITERS
        if not last_turn:
            raw = transposed_part(left_rays, left_faces) - beta_value * right_vector
            full_model, right_vector, alpha_new = normalized_field(raw)
        rho_value = jnp.sqrt(rho_bar * rho_bar + beta_value * beta_value)
        cosine = rho_bar / rho_value
        sine_value = beta_value / rho_value
        phi_value = cosine * phi_bar
        phi_bar = sine_value * phi_bar
        solution = solution + phi_value / rho_value * direction
        if not last_turn:
            rho_bar = -cosine * alpha_new
            direction = right_vector - sine_value * alpha_new / rho_value * direction
            alpha_value = alpha_new
    return solution


def solution(mesh):
    in_specs = (
        P("dp", None),
        P("dp", "region", None, None),
        P("dp", "region"),
        P(("dp", "region"), None),
        P(("dp", "region"), None),
        P(("dp", "region")),
    )
    out_specs = P("region", None)
    return jax.shard_map(local, mesh=mesh, in_specs=in_specs, out_specs=out_specs, check_vma=False)
```

```python
import jax
import jax.numpy as jnp
from jax import lax
from jax.sharding import PartitionSpec as P

ITERS = 2
NB_DEV = 256


smooth_weight = 1.0


def butterfly_sum(x, axis, reverse=False):
    n = lax.axis_size(axis)
    if n & (n - 1):
        return lax.psum(x, axis)
    steps = [1 << j for j in range(n.bit_length() - 1)]
    for k in steps[::-1] if reverse else steps:
        x = x + lax.ppermute(x, axis, [(i, i ^ k) for i in range(n)])
    return x


def square_sum(rows, axis):
    n = lax.psum(1, axis)
    squares = rows * rows
    spread = jnp.dot(
        jnp.ones((n, squares.shape[0]), jnp.float32), squares, precision=lax.Precision.HIGHEST
    )
    got = lax.all_to_all(spread[:, None, :], axis, 0, 0, tiled=False)
    total = got[0]
    for j in range(1, n):
        total = total + got[j]
    return jnp.sum(total)


def halving_scatter(x, axis):
    n = lax.axis_size(axis)
    if n & (n - 1):
        summed = lax.psum(x, axis)
        rows = x.shape[0] // n
        return lax.dynamic_slice_in_dim(summed, lax.axis_index(axis) * rows, rows, 0)
    me = lax.axis_index(axis)
    levels = n.bit_length() - 1
    x = x.reshape((2,) * levels + (x.shape[0] // n,) + x.shape[1:])
    k = 1
    while k < n:
        place = x.ndim - 3
        bit = (me // k) % 2
        keep = lax.dynamic_index_in_dim(x, bit, place, keepdims=False)
        send = lax.dynamic_index_in_dim(x, 1 - bit, place, keepdims=False)
        x = keep + lax.ppermute(send, axis, [(i, i ^ k) for i in range(n)])
        k *= 2
    return x


def doubling_gather(x, axis):
    n = lax.axis_size(axis)
    if n & (n - 1):
        return lax.all_gather(x, axis, axis=0, tiled=True)
    me = lax.axis_index(axis)
    rows = x.shape[0]
    k = n // 2
    while k >= 1:
        other = lax.ppermute(x, axis, [(i, i ^ k) for i in range(n)])
        upper = (me // k) % 2 == 1
        place = x.ndim - 2
        x = jnp.where(upper, jnp.stack([other, x], place), jnp.stack([x, other], place))
        k //= 2
    return x.reshape((n * rows,) + x.shape[-1:])


def local(travel_times, sensitivity, tile_blocks, face_blocks, face_weights, face_count):
    n_region = lax.axis_size("region")
    model_rows = NB_DEV * n_region
    region = lax.axis_index("region")
    live_mask = (jnp.arange(face_blocks.shape[0]) < face_count[0]).astype(jnp.float32)
    face_scale = smooth_weight * face_weights * live_mask[:, None]
    first_block = face_blocks[:, 0]
    second_block = face_blocks[:, 1]
    flat_blocks = tile_blocks.reshape(-1)
    n_tiles = travel_times.shape[0]
    columns = jnp.arange(model_rows, dtype=jnp.int32)[None, :]
    select = jnp.concatenate(
        [
            (flat_blocks[:, None] == columns).astype(jnp.float32),
            (first_block[:, None] == columns).astype(jnp.float32)
            - (second_block[:, None] == columns).astype(jnp.float32),
        ],
        0,
    )
    select_half = select.astype(jnp.bfloat16)
    select_triple = jnp.concatenate([select_half] * 3, 0)
    n_slots = flat_blocks.shape[0]

    def transposed_part(left_rays, left_faces):
        rays_half = left_rays.astype(jnp.bfloat16)
        contrib = jnp.einsum(
            "tsrb,tr->tsb", sensitivity, rays_half, preferred_element_type=jnp.float32
        )
        contrib_rows = contrib.reshape(-1, contrib.shape[-1])
        face_term = face_scale * left_faces
        terms = jnp.concatenate([contrib_rows, face_term], 0)
        high_wide = lax.reduce_precision(terms, exponent_bits=8, mantissa_bits=7)
        rest = terms - high_wide
        middle_wide = lax.reduce_precision(rest, exponent_bits=8, mantissa_bits=7)
        high = high_wide.astype(jnp.bfloat16)
        middle = middle_wide.astype(jnp.bfloat16)
        low = (rest - middle_wide).astype(jnp.bfloat16)
        partials = lax.dot_general(
            select_triple,
            jnp.concatenate([high, middle, low], 0),
            (((0,), (0,)), ((), ())),
            preferred_element_type=jnp.float32,
        )
        piece = halving_scatter(partials, "region")
        return butterfly_sum(piece, "dp")

    def normalized_field(piece):
        field = doubling_gather(piece, "region")
        alpha = jnp.sqrt(jnp.sum(field * field))
        field = field / alpha
        return field, lax.dynamic_slice_in_dim(field, region * NB_DEV, NB_DEV, 0), alpha

    beta_value = jnp.sqrt(square_sum(travel_times, "dp"))
    left_rays = travel_times / beta_value
    left_faces = jnp.zeros(face_weights.shape, jnp.float32)
    raw = transposed_part(left_rays, left_faces)
    full_model, right_vector, alpha_value = normalized_field(raw)
    direction = right_vector
    solution = jnp.zeros_like(right_vector)
    phi_bar = beta_value
    rho_bar = alpha_value
    for iteration in range(ITERS):
        full_half = full_model.astype(jnp.bfloat16)
        rows = jnp.dot(select_half, full_half, preferred_element_type=jnp.float32)
        picked = rows[:n_slots].astype(jnp.bfloat16).reshape(tile_blocks.shape + rows.shape[-1:])
        half_tiles = n_tiles // 2 if n_tiles % 16 == 0 else n_tiles
        halves = []
        for lo in range(0, n_tiles, half_tiles):
            part = jnp.einsum(
                "tsrb,tsb->tr",
                sensitivity[lo:lo + half_tiles],
                picked[lo:lo + half_tiles],
                preferred_element_type=jnp.float32,
            )
            halves.append(butterfly_sum(part, "region", reverse=len(halves) % 2 == 1))
        ray_pred = jnp.concatenate(halves, 0) if len(halves) > 1 else halves[0]
        face_pred = face_scale * rows[n_slots:]
        left_faces = face_pred - alpha_value * left_faces
        left_rays = ray_pred - alpha_value * left_rays
        if n_tiles % n_region == 0:
            share = n_tiles // n_region
            own_rays = lax.dynamic_slice_in_dim(left_rays, region * share, share, 0)
        else:
            own_rays = jnp.where(region == 0, left_rays, 0.0)
        beta_sq = square_sum(jnp.concatenate([own_rays, left_faces], 0), ("dp", "region"))
        beta_value = jnp.sqrt(beta_sq)
        left_rays = left_rays / beta_value
        left_faces = left_faces / beta_value
        last_turn = iteration + 1 == ITERS
        if not last_turn:
            raw = transposed_part(left_rays, left_faces) - beta_value * right_vector
            full_model, right_vector, alpha_new = normalized_field(raw)
        rho_value = jnp.sqrt(rho_bar * rho_bar + beta_value * beta_value)
        cosine = rho_bar / rho_value
        sine_value = beta_value / rho_value
        phi_value = cosine * phi_bar
        phi_bar = sine_value * phi_bar
        solution = solution + phi_value / rho_value * direction
        if not last_turn:
            rho_bar = -cosine * alpha_new
            direction = right_vector - sine_value * alpha_new / rho_value * direction
            alpha_value = alpha_new
    return solution


def solution(mesh):
    in_specs = (
        P("dp", None),
        P("dp", "region", None, None),
        P("dp", "region"),
        P(("dp", "region"), None),
        P(("dp", "region"), None),
        P(("dp", "region")),
    )
    out_specs = P("region", None)
    return jax.shard_map(local, mesh=mesh, in_specs=in_specs, out_specs=out_specs, check_vma=False)
```

```python
import jax
import jax.numpy as jnp
from jax import lax
from jax.sharding import PartitionSpec as P

ITERS = 2
NB_DEV = 256


smooth_weight = 1.0


def butterfly_sum(x, axis):
    n = lax.axis_size(axis)
    if n & (n - 1):
        return lax.psum(x, axis)
    k = 1
    while k < n:
        x = x + lax.ppermute(x, axis, [(i, i ^ k) for i in range(n)])
        k *= 2
    return x


def square_sum(rows, axis):
    n = lax.psum(1, axis)
    squares = rows * rows
    spread = jnp.dot(
        jnp.ones((n, squares.shape[0]), jnp.float32), squares, precision=lax.Precision.HIGHEST
    )
    got = lax.all_to_all(spread[:, None, :], axis, 0, 0, tiled=False)
    total = got[0]
    for j in range(1, n):
        total = total + got[j]
    return jnp.sum(total)


def halving_scatter(x, axis):
    n = lax.axis_size(axis)
    if n & (n - 1):
        summed = lax.psum(x, axis)
        rows = x.shape[0] // n
        return lax.dynamic_slice_in_dim(summed, lax.axis_index(axis) * rows, rows, 0)
    me = lax.axis_index(axis)
    levels = n.bit_length() - 1
    x = x.reshape((2,) * levels + (x.shape[0] // n,) + x.shape[1:])
    k = 1
    while k < n:
        place = x.ndim - 3
        bit = (me // k) % 2
        keep = lax.dynamic_index_in_dim(x, bit, place, keepdims=False)
        send = lax.dynamic_index_in_dim(x, 1 - bit, place, keepdims=False)
        x = keep + lax.ppermute(send, axis, [(i, i ^ k) for i in range(n)])
        k *= 2
    return x


def doubling_gather(x, axis):
    n = lax.axis_size(axis)
    if n & (n - 1):
        return lax.all_gather(x, axis, axis=0, tiled=True)
    me = lax.axis_index(axis)
    rows = x.shape[0]
    k = n // 2
    while k >= 1:
        other = lax.ppermute(x, axis, [(i, i ^ k) for i in range(n)])
        upper = (me // k) % 2 == 1
        place = x.ndim - 2
        x = jnp.where(upper, jnp.stack([other, x], place), jnp.stack([x, other], place))
        k //= 2
    return x.reshape((n * rows,) + x.shape[-1:])


def gather_with_norm(x, axis):
    n = lax.axis_size(axis)
    if n & (n - 1):
        field = lax.all_gather(x, axis, axis=0, tiled=True)
        return field, jnp.sum(field * field)
    me = lax.axis_index(axis)
    rows = x.shape[0]
    sums = jnp.sum(x * x, axis=(-2, -1))
    k = n // 2
    while k >= 1:
        other = lax.ppermute(x, axis, [(i, i ^ k) for i in range(n)])
        other_sums = jnp.sum(other * other, axis=(-2, -1))
        upper = (me // k) % 2 == 1
        place = x.ndim - 2
        x = jnp.where(upper, jnp.stack([other, x], place), jnp.stack([x, other], place))
        sums = jnp.where(upper, jnp.stack([other_sums, sums], place), jnp.stack([sums, other_sums], place))
        k //= 2
    sums = sums.reshape(n)
    total = sums[0]
    for j in range(1, n):
        total = total + sums[j]
    return x.reshape((n * rows,) + x.shape[-1:]), total


def local(travel_times, sensitivity, tile_blocks, face_blocks, face_weights, face_count):
    n_region = lax.axis_size("region")
    model_rows = NB_DEV * n_region
    region = lax.axis_index("region")
    live_mask = (jnp.arange(face_blocks.shape[0]) < face_count[0]).astype(jnp.float32)
    face_scale = smooth_weight * face_weights * live_mask[:, None]
    first_block = face_blocks[:, 0]
    second_block = face_blocks[:, 1]
    flat_blocks = tile_blocks.reshape(-1)
    n_tiles = travel_times.shape[0]
    columns = jnp.arange(model_rows, dtype=jnp.int32)[None, :]
    select = jnp.concatenate(
        [
            (flat_blocks[:, None] == columns).astype(jnp.float32),
            (first_block[:, None] == columns).astype(jnp.float32)
            - (second_block[:, None] == columns).astype(jnp.float32),
        ],
        0,
    )
    select_half = select.astype(jnp.bfloat16)
    select_triple = jnp.concatenate([select_half] * 3, 0)
    n_slots = flat_blocks.shape[0]

    def transposed_part(left_rays, left_faces):
        rays_half = left_rays.astype(jnp.bfloat16)
        contrib = jnp.einsum(
            "tsrb,tr->tsb", sensitivity, rays_half, preferred_element_type=jnp.float32
        )
        contrib_rows = contrib.reshape(-1, contrib.shape[-1])
        face_term = face_scale * left_faces
        terms = jnp.concatenate([contrib_rows, face_term], 0)
        high_wide = lax.reduce_precision(terms, exponent_bits=8, mantissa_bits=7)
        rest = terms - high_wide
        middle_wide = lax.reduce_precision(rest, exponent_bits=8, mantissa_bits=7)
        high = high_wide.astype(jnp.bfloat16)
        middle = middle_wide.astype(jnp.bfloat16)
        low = (rest - middle_wide).astype(jnp.bfloat16)
        partials = lax.dot_general(
            select_triple,
            jnp.concatenate([high, middle, low], 0),
            (((0,), (0,)), ((), ())),
            preferred_element_type=jnp.float32,
        )
        piece = halving_scatter(partials, "region")
        return butterfly_sum(piece, "dp")

    def normalized_field(piece):
        field, squares = gather_with_norm(piece, "region")
        alpha = jnp.sqrt(squares)
        field = field / alpha
        return field, lax.dynamic_slice_in_dim(field, region * NB_DEV, NB_DEV, 0), alpha

    beta_value = jnp.sqrt(square_sum(travel_times, "dp"))
    left_rays = travel_times / beta_value
    left_faces = jnp.zeros(face_weights.shape, jnp.float32)
    raw = transposed_part(left_rays, left_faces)
    full_model, right_vector, alpha_value = normalized_field(raw)
    direction = right_vector
    solution = jnp.zeros_like(right_vector)
    phi_bar = beta_value
    rho_bar = alpha_value
    for iteration in range(ITERS):
        full_half = full_model.astype(jnp.bfloat16)
        rows = jnp.dot(select_half, full_half, preferred_element_type=jnp.float32)
        picked = rows[:n_slots].astype(jnp.bfloat16).reshape(tile_blocks.shape + rows.shape[-1:])
        half_tiles = n_tiles // 2 if n_tiles % 16 == 0 else n_tiles
        halves = []
        for lo in range(0, n_tiles, half_tiles):
            part = jnp.einsum(
                "tsrb,tsb->tr",
                sensitivity[lo:lo + half_tiles],
                picked[lo:lo + half_tiles],
                preferred_element_type=jnp.float32,
            )
            halves.append(butterfly_sum(part, "region"))
        ray_pred = jnp.concatenate(halves, 0) if len(halves) > 1 else halves[0]
        face_pred = face_scale * rows[n_slots:]
        left_faces = face_pred - alpha_value * left_faces
        left_rays = ray_pred - alpha_value * left_rays
        if n_tiles % n_region == 0:
            share = n_tiles // n_region
            own_rays = lax.dynamic_slice_in_dim(left_rays, region * share, share, 0)
        else:
            own_rays = jnp.where(region == 0, left_rays, 0.0)
        beta_sq = square_sum(jnp.concatenate([own_rays, left_faces], 0), ("dp", "region"))
        beta_value = jnp.sqrt(beta_sq)
        left_rays = left_rays / beta_value
        left_faces = left_faces / beta_value
        last_turn = iteration + 1 == ITERS
        if not last_turn:
            raw = transposed_part(left_rays, left_faces) - beta_value * right_vector
            full_model, right_vector, alpha_new = normalized_field(raw)
        rho_value = jnp.sqrt(rho_bar * rho_bar + beta_value * beta_value)
        cosine = rho_bar / rho_value
        sine_value = beta_value / rho_value
        phi_value = cosine * phi_bar
        phi_bar = sine_value * phi_bar
        solution = solution + phi_value / rho_value * direction
        if not last_turn:
            rho_bar = -cosine * alpha_new
            direction = right_vector - sine_value * alpha_new / rho_value * direction
            alpha_value = alpha_new
    return solution


def solution(mesh):
    in_specs = (
        P("dp", None),
        P("dp", "region", None, None),
        P("dp", "region"),
        P(("dp", "region"), None),
        P(("dp", "region"), None),
        P(("dp", "region")),
    )
    out_specs = P("region", None)
    return jax.shard_map(local, mesh=mesh, in_specs=in_specs, out_specs=out_specs, check_vma=False)
```

```python
import jax
import jax.numpy as jnp
from jax import lax
from jax.sharding import PartitionSpec as P

ITERS = 2
NB_DEV = 256


smooth_weight = 1.0


def butterfly_sum(x, axis, first=1):
    n = lax.axis_size(axis)
    if n & (n - 1):
        return lax.psum(x, axis)
    steps = [1 << j for j in range(n.bit_length() - 1)]
    if first in steps:
        steps.remove(first)
        steps.insert(0, first)
    for k in steps:
        x = x + lax.ppermute(x, axis, [(i, i ^ k) for i in range(n)])
    return x


def square_sum(rows, axis):
    n = lax.psum(1, axis)
    squares = rows * rows
    spread = jnp.dot(
        jnp.ones((n, squares.shape[0]), jnp.float32), squares, precision=lax.Precision.HIGHEST
    )
    got = lax.all_to_all(spread[:, None, :], axis, 0, 0, tiled=False)
    total = got[0]
    for j in range(1, n):
        total = total + got[j]
    return jnp.sum(total)


def halving_scatter(x, axis):
    n = lax.axis_size(axis)
    if n & (n - 1):
        summed = lax.psum(x, axis)
        rows = x.shape[0] // n
        return lax.dynamic_slice_in_dim(summed, lax.axis_index(axis) * rows, rows, 0)
    me = lax.axis_index(axis)
    levels = n.bit_length() - 1
    x = x.reshape((2,) * levels + (x.shape[0] // n,) + x.shape[1:])
    k = 1
    while k < n:
        place = x.ndim - 3
        bit = (me // k) % 2
        keep = lax.dynamic_index_in_dim(x, bit, place, keepdims=False)
        send = lax.dynamic_index_in_dim(x, 1 - bit, place, keepdims=False)
        x = keep + lax.ppermute(send, axis, [(i, i ^ k) for i in range(n)])
        k *= 2
    return x


def doubling_gather(x, axis):
    n = lax.axis_size(axis)
    if n & (n - 1):
        return lax.all_gather(x, axis, axis=0, tiled=True)
    me = lax.axis_index(axis)
    rows = x.shape[0]
    k = n // 2
    while k >= 1:
        other = lax.ppermute(x, axis, [(i, i ^ k) for i in range(n)])
        upper = (me // k) % 2 == 1
        place = x.ndim - 2
        x = jnp.where(upper, jnp.stack([other, x], place), jnp.stack([x, other], place))
        k //= 2
    return x.reshape((n * rows,) + x.shape[-1:])


def local(travel_times, sensitivity, tile_blocks, face_blocks, face_weights, face_count):
    n_region = lax.axis_size("region")
    model_rows = NB_DEV * n_region
    region = lax.axis_index("region")
    live_mask = (jnp.arange(face_blocks.shape[0]) < face_count[0]).astype(jnp.float32)
    face_scale = smooth_weight * face_weights * live_mask[:, None]
    first_block = face_blocks[:, 0]
    second_block = face_blocks[:, 1]
    flat_blocks = tile_blocks.reshape(-1)
    n_tiles = travel_times.shape[0]
    columns = jnp.arange(model_rows, dtype=jnp.int32)[None, :]
    select = jnp.concatenate(
        [
            (flat_blocks[:, None] == columns).astype(jnp.float32),
            (first_block[:, None] == columns).astype(jnp.float32)
            - (second_block[:, None] == columns).astype(jnp.float32),
        ],
        0,
    )
    select_half = select.astype(jnp.bfloat16)
    select_triple = jnp.concatenate([select_half] * 3, 0)
    n_slots = flat_blocks.shape[0]

    def transposed_part(left_rays, left_faces):
        rays_half = left_rays.astype(jnp.bfloat16)
        contrib = jnp.einsum(
            "tsrb,tr->tsb", sensitivity, rays_half, preferred_element_type=jnp.float32
        )
        contrib_rows = contrib.reshape(-1, contrib.shape[-1])
        face_term = face_scale * left_faces
        terms = jnp.concatenate([contrib_rows, face_term], 0)
        high_wide = lax.reduce_precision(terms, exponent_bits=8, mantissa_bits=7)
        rest = terms - high_wide
        middle_wide = lax.reduce_precision(rest, exponent_bits=8, mantissa_bits=7)
        high = high_wide.astype(jnp.bfloat16)
        middle = middle_wide.astype(jnp.bfloat16)
        low = (rest - middle_wide).astype(jnp.bfloat16)
        partials = lax.dot_general(
            select_triple,
            jnp.concatenate([high, middle, low], 0),
            (((0,), (0,)), ((), ())),
            preferred_element_type=jnp.float32,
        )
        piece = halving_scatter(partials, "region")
        return butterfly_sum(piece, "dp", first=2)

    def normalized_field(piece):
        field = doubling_gather(piece, "region")
        alpha = jnp.sqrt(jnp.sum(field * field))
        field = field / alpha
        return field, lax.dynamic_slice_in_dim(field, region * NB_DEV, NB_DEV, 0), alpha

    beta_value = jnp.sqrt(square_sum(travel_times, "dp"))
    left_rays = travel_times / beta_value
    left_faces = jnp.zeros(face_weights.shape, jnp.float32)
    raw = transposed_part(left_rays, left_faces)
    full_model, right_vector, alpha_value = normalized_field(raw)
    direction = right_vector
    solution = jnp.zeros_like(right_vector)
    phi_bar = beta_value
    rho_bar = alpha_value
    for iteration in range(ITERS):
        full_half = full_model.astype(jnp.bfloat16)
        rows = jnp.dot(select_half, full_half, preferred_element_type=jnp.float32)
        picked = rows[:n_slots].astype(jnp.bfloat16).reshape(tile_blocks.shape + rows.shape[-1:])
        half_tiles = n_tiles // 2 if n_tiles % 16 == 0 else n_tiles
        halves = []
        for lo in range(0, n_tiles, half_tiles):
            part = jnp.einsum(
                "tsrb,tsb->tr",
                sensitivity[lo:lo + half_tiles],
                picked[lo:lo + half_tiles],
                preferred_element_type=jnp.float32,
            )
            halves.append(butterfly_sum(part, "region"))
        ray_pred = jnp.concatenate(halves, 0) if len(halves) > 1 else halves[0]
        face_pred = face_scale * rows[n_slots:]
        left_faces = face_pred - alpha_value * left_faces
        left_rays = ray_pred - alpha_value * left_rays
        if n_tiles % n_region == 0:
            share = n_tiles // n_region
            own_rays = lax.dynamic_slice_in_dim(left_rays, region * share, share, 0)
        else:
            own_rays = jnp.where(region == 0, left_rays, 0.0)
        beta_sq = square_sum(jnp.concatenate([own_rays, left_faces], 0), ("dp", "region"))
        beta_value = jnp.sqrt(beta_sq)
        left_rays = left_rays / beta_value
        left_faces = left_faces / beta_value
        last_turn = iteration + 1 == ITERS
        if not last_turn:
            raw = transposed_part(left_rays, left_faces) - beta_value * right_vector
            full_model, right_vector, alpha_new = normalized_field(raw)
        rho_value = jnp.sqrt(rho_bar * rho_bar + beta_value * beta_value)
        cosine = rho_bar / rho_value
        sine_value = beta_value / rho_value
        phi_value = cosine * phi_bar
        phi_bar = sine_value * phi_bar
        solution = solution + phi_value / rho_value * direction
        if not last_turn:
            rho_bar = -cosine * alpha_new
            direction = right_vector - sine_value * alpha_new / rho_value * direction
            alpha_value = alpha_new
    return solution


def solution(mesh):
    in_specs = (
        P("dp", None),
        P("dp", "region", None, None),
        P("dp", "region"),
        P(("dp", "region"), None),
        P(("dp", "region"), None),
        P(("dp", "region")),
    )
    out_specs = P("region", None)
    return jax.shard_map(local, mesh=mesh, in_specs=in_specs, out_specs=out_specs, check_vma=False)
```
